512 devices in a mesh: dp: 8 (over x, core), expert: 64 (over z, y).
Axes of the slice: x: 4, y: 4, z: 16, core: 2. Of those that a mesh axis runs over, the one named last changes fastest.
Arguments:
- tokens_in: bfloat16 [8192, 2048], P(('dp', 'expert')), may hold values from -6 to 6
- out_grad: bfloat16 [8192, 2048], P(('dp', 'expert')), may hold values from -6 to 6
- chosen: int32 [8, 32, 64], P('dp'), may hold values from 0 to 1023, as said below
- counts: int32 [8, 32], P('dp'), may hold values from 48 to 64, as said below
- gates: bfloat16 [8, 32, 64], P('dp'), may hold values from 0.049804688 to 1
- w_up: bfloat16 [64, 2048, 2048], P('expert', None, 'dp'), may hold values from -0.125 to 0.125
- w_down: bfloat16 [64, 2048, 2048], P('expert', 'dp'), may hold values from -0.09375 to 0.09375
Outputs:
- in_grad: bfloat16 [8192, 2048], P(('dp', 'expert'))
- grad_up: bfloat16 [64, 2048, 2048], P('expert', None, 'dp')
- grad_down: bfloat16 [64, 2048, 2048], P('expert', 'dp')
- gate_grad: float32 [8, 64, 32], P('dp', 'expert')
The draws below stay inside these ranges and needn't reach their ends.
Inputs may be any that keep to these rules, and one draw needn't show every extreme that they name: chosen[g, e, c] numbers a token within group g; that token lives on index chosen[g, e, c] // 16 of the expert axis. One list names no token twice. Among the first 32 slots of a list no two tokens live on the same index of the expert axis, nor among the last 32; so one expert takes at most 2 tokens of one device, and some device gives 2 to an expert in every list. Slots at or beyond counts[g, e] are ignored. `counts`: in every group some expert has all its slots valid.
All inputs are finite; a program needn't handle non-finite values.
Results may differ from the reference program's by a relative error of at most 0.028.
Values may be sent and summed in bfloat16 or wider, within the bound.
No kernel may reach another device: no remote copies, remote signals or barrier semaphores. Data moves between devices by JAX's collectives and lax.ppermute only.
A program may use at most 64 MiB of HBM per device.

```python
import math
import jax
import jax.numpy as jnp
from jax import lax

D = 2048
FF = 4096
TOK_DEV = 16
OWNERS = 64
EXPERTS = 32
GROUPS = 8
CAP = 64
HIDDEN_DEV = 256
TOKENS = 8192
N_DP = 8


def one_list(list_key):
    half_cap = CAP // 2
    subkeys = jax.random.split(list_key, 5)
    order_one = jax.random.permutation(subkeys[0], OWNERS).astype(jnp.int32)
    order_two = jax.random.permutation(subkeys[1], OWNERS).astype(jnp.int32)
    spot_index = jax.random.randint(subkeys[2], (), 0, CAP // 4)
    target = order_one[spot_index]
    positions = jnp.arange(OWNERS, dtype=jnp.int32)
    order_two = jnp.where(order_two == target, order_two[spot_index], jnp.where(positions == spot_index, target, order_two))
    local_one = jax.random.randint(subkeys[3], (OWNERS,), 0, TOK_DEV)
    offset = jax.random.randint(subkeys[4], (OWNERS,), 1, TOK_DEV)
    local_two = (local_one + offset) % TOK_DEV
    front_owner = order_one[:half_cap]
    back_owner = order_two[:half_cap]
    front_rows = front_owner * TOK_DEV + local_one[front_owner]
    back_rows = back_owner * TOK_DEV + local_two[back_owner]
    return jnp.concatenate([front_rows, back_rows]).astype(jnp.int32)


def draw_chosen(key, part):
    subkeys = jax.random.split(jax.random.fold_in(key, 11), GROUPS * EXPERTS)
    all_lists = jax.vmap(one_list)(subkeys)
    return all_lists.reshape(GROUPS, EXPERTS, CAP).astype(jnp.int32)


def draw_counts(key, part):
    subkeys = jax.random.split(jax.random.fold_in(key, 23), 2)
    drawn = jax.random.randint(subkeys[0], (GROUPS, EXPERTS), CAP - CAP // 4, CAP + 1)
    full_expert = jax.random.randint(subkeys[1], (GROUPS, 1), 0, EXPERTS)
    expert_ids = jnp.arange(EXPERTS, dtype=jnp.int32)[None, :]
    return jnp.where(expert_ids == full_expert, CAP, drawn).astype(jnp.int32)


def level_of(own_key, dims, cuts, smallest, largest):
    level = 1.0
    for dim, blocks in cuts:
        draws = jax.random.uniform(jax.random.fold_in(jax.random.fold_in(own_key, 6), dim), (blocks,), jnp.float32, smallest / len(cuts), largest / len(cuts))
        level = level * jnp.repeat(jnp.exp(draws), dims[dim] // blocks).reshape((-1,) + (1,) * (len(dims) - 1 - dim))
    return level


def scatter_about(own_key, dims, width, most, cuts=(), kind=jnp.bfloat16):
    factor_of = level_of(own_key, dims, cuts, -0.22, 0.18) if cuts else 1.0
    result = jax.random.normal(own_key, dims, jnp.float32) * width * factor_of
    return jnp.minimum(jnp.maximum(result, -most), most).astype(kind)


def setup_inputs(seed: int = 0) -> dict:
    splits = jax.random.split(jax.random.key(seed), 8)
    tokens_in = scatter_about(splits[0], (TOKENS, D), 1.0, 6.0, ((0, 512),))
    out_grad = scatter_about(splits[1], (TOKENS, D), 1.0, 6.0, ((0, 512),))
    chosen = draw_chosen(jax.random.fold_in(splits[7], 71), 0)
    counts = draw_counts(jax.random.fold_in(splits[7], 71), 0)
    gates = jnp.clip(jnp.exp(math.log(1.0) - 2.9996462 * jax.random.uniform(splits[4], (GROUPS, EXPERTS, CAP), jnp.float32) ** level_of(splits[4], (GROUPS, EXPERTS, CAP), ((0, 8),), -0.2, 0.2)), 0.049804688, 1.0).astype(jnp.bfloat16)
    w_up = scatter_about(splits[5], (2 * EXPERTS, D, FF // 2), D ** -0.5, 0.125, ((0, 64), (2, 8)))
    w_down = scatter_about(splits[6], (2 * EXPERTS, FF // 2, D), FF ** -0.5, 0.09375, ((0, 64), (1, 8)))
    return {"tokens_in": tokens_in, "out_grad": out_grad, "chosen": chosen, "counts": counts, "gates": gates, "w_up": w_up, "w_down": w_down}


root_two_over_pi = 0.7978845608028654
cubic_coef = 0.044715


def gelu_pair(pre_act):
    inner_arg = root_two_over_pi * (pre_act + cubic_coef * pre_act * pre_act * pre_act)
    tangent = jnp.tanh(inner_arg)
    act_value = 0.5 * pre_act * (1.0 + tangent)
    act_slope = 0.5 * (1.0 + tangent) + 0.5 * pre_act * (1.0 - tangent * tangent) * root_two_over_pi * (1.0 + 3.0 * cubic_coef * pre_act * pre_act)
    return act_value, act_slope


def to_low(values):
    return lax.optimization_barrier(values.astype(jnp.bfloat16)).astype(jnp.float32)


def reference(tokens_in, out_grad, chosen, counts, gates, w_up, w_down):
    group_size = TOK_DEV * OWNERS
    slices = 2 * N_DP
    offsets = (jnp.arange(GROUPS, dtype=jnp.int32) * group_size)[:, None]
    slot_ids = jnp.arange(CAP, dtype=jnp.int32)[None, :]

    def per_expert(grad_acc, expert):
        row_ids = (chosen[:, expert, :] + offsets).astype(jnp.int32)
        is_valid = slot_ids < counts[:, expert][:, None]
        valid_float = is_valid.astype(jnp.float32)
        weight = jnp.where(is_valid, gates[:, expert, :].astype(jnp.float32), jnp.zeros((), jnp.float32))
        token_rows = tokens_in[row_ids].astype(jnp.float32)
        grad_rows = out_grad[row_ids].astype(jnp.float32)
        up_full = jnp.concatenate([w_up[2 * expert], w_up[2 * expert + 1]], axis=1).astype(jnp.float32)
        down_full = jnp.concatenate([w_down[2 * expert], w_down[2 * expert + 1]], axis=0).astype(jnp.float32)
        pre_act = jnp.einsum("gcd,df->gcf", token_rows, up_full)
        act_value, act_slope = gelu_pair(pre_act)
        hidden = to_low(act_value)
        back_grad = jnp.einsum("gcd,fd->gcf", grad_rows, down_full)
        scaled = to_low(weight[:, :, None] * grad_rows)
        pre_grad = to_low(weight[:, :, None] * back_grad * act_slope)
        grad_down = jnp.einsum("gcf,gcd->fd", hidden, scaled).astype(jnp.bfloat16)
        grad_up = jnp.einsum("gcd,gcf->df", token_rows, pre_grad).astype(jnp.bfloat16)
        split_grad = pre_grad.reshape(GROUPS, CAP, slices, HIDDEN_DEV)
        split_up = up_full.reshape(D, slices, HIDDEN_DEV)
        pieces = to_low(jnp.einsum("gcsh,dsh->gcsd", split_grad, split_up))
        contrib = jnp.sum(pieces, axis=2) * valid_float[:, :, None]
        gate_pieces = to_low(jnp.sum((hidden * back_grad).reshape(GROUPS, CAP, slices, HIDDEN_DEV), axis=3))
        gate_grad = jnp.sum(gate_pieces, axis=2) * valid_float
        grad_acc = grad_acc.at[row_ids.reshape(-1)].add(contrib.reshape(-1, D))
        up_halves = jnp.transpose(grad_up.reshape(D, 2, FF // 2), (1, 0, 2))
        down_halves = grad_down.reshape(2, FF // 2, D)
        return grad_acc, (up_halves, down_halves, gate_grad.reshape(GROUPS, 2, CAP // 2))

    start_acc = jnp.zeros((TOKENS, D), jnp.float32)
    grad_acc, (up_all, down_all, gate_all) = lax.scan(per_expert, start_acc, jnp.arange(EXPERTS, dtype=jnp.int32))
    in_grad = grad_acc.astype(jnp.bfloat16)
    grad_up = up_all.reshape(2 * EXPERTS, D, FF // 2)
    grad_down = down_all.reshape(2 * EXPERTS, FF // 2, D)
    gate_grad = jnp.transpose(gate_all, (1, 0, 2, 3)).reshape(GROUPS, 2 * EXPERTS, CAP // 2)
    return (in_grad, grad_up, grad_down, gate_grad)
```

```python
import jax
import jax.numpy as jnp
from jax import lax
from jax.sharding import PartitionSpec as P

root_two_over_pi = 0.7978845608028654
cubic_coef = 0.044715


def partner(x, axis, apart):
    return lax.ppermute(x, axis, [(i, i ^ 1 << apart) for i in range(lax.axis_size(axis))])


def gelu_pair(pre_act):
    inner_arg = root_two_over_pi * (pre_act + cubic_coef * pre_act * pre_act * pre_act)
    tangent = jnp.tanh(inner_arg)
    act_value = 0.5 * pre_act * (1.0 + tangent)
    act_slope = 0.5 * (1.0 + tangent) + 0.5 * pre_act * (
        1.0 - tangent * tangent
    ) * root_two_over_pi * (1.0 + 3.0 * cubic_coef * pre_act * pre_act)
    return (act_value, act_slope)


def on_device(tokens_in, out_grad, chosen, counts, gates, w_up, w_down):
    tok_local = tokens_in.shape[0]
    width = tokens_in.shape[1]
    owners = lax.axis_size("expert")
    groups = lax.axis_size("dp")
    capacity = chosen.shape[2]
    half_cap = capacity // 2
    num_experts = chosen.shape[1]
    device = lax.axis_index("expert")
    expert = device // 2
    parity = device % 2
    highest = lax.Precision.HIGHEST
    my_lists = chosen[0]
    slot_ids = jnp.arange(capacity, dtype=jnp.int32)
    is_valid = slot_ids[None, :] < counts[0][:, None]
    owner_of = my_lists // tok_local
    local_of = my_lists % tok_local
    mine = jnp.logical_and(owner_of == device, is_valid)
    local_ids = jnp.arange(tok_local, dtype=jnp.int32)
    hits = jnp.logical_and(mine[:, :, None], local_of[:, :, None] == local_ids[None, None, :])
    picked = jnp.sum(hits.astype(jnp.float32).reshape(num_experts, 2, half_cap, tok_local), axis=2)
    picked_low = picked.astype(jnp.bfloat16)
    list_row = lax.dynamic_index_in_dim(my_lists, expert, 0, keepdims=False)
    count_here = lax.dynamic_index_in_dim(counts[0], expert, 0, keepdims=False)
    valid_here = slot_ids < count_here
    gate_here = jnp.where(
        valid_here,
        lax.dynamic_index_in_dim(gates[0], expert, 0, keepdims=False),
        jnp.zeros((), jnp.bfloat16),
    )
    owner_ids = jnp.arange(owners, dtype=jnp.int32)
    slot_map = jnp.logical_and(
        (list_row // tok_local)[:, None] == owner_ids[None, :], valid_here[:, None]
    )
    slot_map = slot_map.astype(jnp.float32).reshape(2, half_cap, owners)
    map_low = slot_map.astype(jnp.bfloat16)
    gate_rows = gate_here.reshape(2, half_cap)
    both = jnp.concatenate([tokens_in, out_grad], axis=1)
    send_xg = jnp.einsum(
        "erl,ld->red", picked_low, both, preferred_element_type=jnp.float32
    ).astype(jnp.bfloat16)
    send_xg = jnp.repeat(send_xg, 2, axis=1)
    recv_xg = lax.all_to_all(send_xg, "expert", split_axis=1, concat_axis=1, tiled=True)
    rows_xg = jnp.einsum(
        "rij,rjd->rid", map_low, recv_xg, preferred_element_type=jnp.float32
    ).astype(jnp.bfloat16)
    gate_col = jnp.pad(gate_rows[:, :, None], ((0, 0), (0, 0), (0, 127)))
    packed = jnp.concatenate([rows_xg, gate_col], axis=2)
    all_p = lax.all_gather(packed, "dp", axis=1, tiled=True)
    flat_x = all_p[:, :, :width].reshape(-1, width)
    flat_g = all_p[:, :, width : 2 * width].reshape(-1, width)
    flat_gate = all_p[:, :, 2 * width].reshape(-1).astype(jnp.float32)
    up_part = w_up[0]
    down_part = w_down[0]
    pre_act = jnp.dot(flat_x, up_part, preferred_element_type=jnp.float32)
    act_value, act_slope = gelu_pair(pre_act)
    hidden = act_value.astype(jnp.bfloat16)
    back_grad = lax.dot_general(
        flat_g, down_part, (((1,), (1,)), ((), ())), preferred_element_type=jnp.float32
    )
    gate_terms = jnp.sum(hidden.astype(jnp.float32) * back_grad, axis=1)
    scaled = (flat_gate[:, None] * flat_g.astype(jnp.float32)).astype(jnp.bfloat16)
    pre_grad = (flat_gate[:, None] * back_grad * act_slope).astype(jnp.bfloat16)
    grad_down = lax.dot_general(
        hidden, scaled, (((0,), (0,)), ((), ())), preferred_element_type=jnp.float32
    )
    grad_up = lax.dot_general(
        flat_x, pre_grad, (((0,), (0,)), ((), ())), preferred_element_type=jnp.float32
    )
    dx_terms = lax.dot_general(
        pre_grad, up_part, (((1,), (1,)), ((), ())), preferred_element_type=jnp.float32
    )
    dx_low = dx_terms.reshape(2, groups * half_cap, width).astype(jnp.bfloat16)
    gate_low = gate_terms.reshape(2, groups * half_cap, 1).astype(jnp.bfloat16)
    gate_low = jnp.pad(gate_low, ((0, 0), (0, 0), (0, 127)))
    reduced = lax.psum_scatter(
        jnp.concatenate([dx_low, gate_low], axis=2),
        "dp",
        scatter_dimension=1,
        tiled=True,
    ).astype(jnp.float32)
    hidden_sum = reduced[:, :, :width]
    gate_sums = reduced[:, :, width]
    spread = jnp.einsum("rij,rid->rjd", slot_map, hidden_sum, precision=highest)
    returned = lax.all_to_all(
        spread.astype(jnp.bfloat16), "expert", split_axis=1, concat_axis=1, tiled=True
    ).astype(spread.dtype)
    take_back = jnp.repeat(picked, 2, axis=0)
    in_grad = jnp.einsum("krl,rkd->ld", take_back, returned, precision=highest)
    partner_gate = partner(gate_sums, "expert", 0)
    gate_total = gate_sums + partner_gate
    gate_out = lax.dynamic_index_in_dim(gate_total, parity, 0, keepdims=False).reshape(
        1, 1, half_cap
    )
    return (
        in_grad.astype(jnp.bfloat16),
        grad_up.astype(jnp.bfloat16)[None],
        grad_down.astype(jnp.bfloat16)[None],
        gate_out,
    )


def solution(mesh):
    placed = (
        P(("dp", "expert"), None),
        P(("dp", "expert"), None),
        P("dp", None, None),
        P("dp", None),
        P("dp", None, None),
        P("expert", None, "dp"),
        P("expert", "dp", None),
    )
    return jax.shard_map(
        on_device,
        mesh=mesh,
        in_specs=placed,
        out_specs=(
            P(("dp", "expert"), None),
            P("expert", None, "dp"),
            P("expert", "dp", None),
            P("dp", "expert", None),
        ),
        check_vma=False,
    )
```

```python
import jax
import jax.numpy as jnp
from jax import lax
from jax.sharding import PartitionSpec as P

root_two_over_pi = 0.7978845608028654
cubic_coef = 0.044715


def partner(x, axis, apart):
    return lax.ppermute(x, axis, [(i, i ^ 1 << apart) for i in range(lax.axis_size(axis))])


def gelu_pair(pre_act):
    inner_arg = root_two_over_pi * (pre_act + cubic_coef * pre_act * pre_act * pre_act)
    tangent = jnp.tanh(inner_arg)
    act_value = 0.5 * pre_act * (1.0 + tangent)
    act_slope = 0.5 * (1.0 + tangent) + 0.5 * pre_act * (
        1.0 - tangent * tangent
    ) * root_two_over_pi * (1.0 + 3.0 * cubic_coef * pre_act * pre_act)
    return (act_value, act_slope)


def on_device(tokens_in, out_grad, chosen, counts, gates, w_up, w_down):
    tok_local = tokens_in.shape[0]
    width = tokens_in.shape[1]
    owners = lax.axis_size("expert")
    groups = lax.axis_size("dp")
    capacity = chosen.shape[2]
    half_cap = capacity // 2
    num_experts = chosen.shape[1]
    device = lax.axis_index("expert")
    expert = device // 2
    parity = device % 2
    highest = lax.Precision.HIGHEST
    my_lists = chosen[0]
    slot_ids = jnp.arange(capacity, dtype=jnp.int32)
    is_valid = slot_ids[None, :] < counts[0][:, None]
    owner_of = my_lists // tok_local
    local_of = my_lists % tok_local
    mine = jnp.logical_and(owner_of == device, is_valid)
    local_ids = jnp.arange(tok_local, dtype=jnp.int32)
    hits = jnp.logical_and(mine[:, :, None], local_of[:, :, None] == local_ids[None, None, :])
    picked = jnp.sum(hits.astype(jnp.float32).reshape(num_experts, 2, half_cap, tok_local), axis=2)
    picked_low = picked.astype(jnp.bfloat16)
    list_row = lax.dynamic_index_in_dim(my_lists, expert, 0, keepdims=False)
    count_here = lax.dynamic_index_in_dim(counts[0], expert, 0, keepdims=False)
    valid_here = slot_ids < count_here
    gate_here = jnp.where(
        valid_here,
        lax.dynamic_index_in_dim(gates[0], expert, 0, keepdims=False),
        jnp.zeros((), jnp.bfloat16),
    )
    owner_ids = jnp.arange(owners, dtype=jnp.int32)
    slot_map = jnp.logical_and(
        (list_row // tok_local)[:, None] == owner_ids[None, :], valid_here[:, None]
    )
    slot_map = slot_map.astype(jnp.float32).reshape(2, half_cap, owners)
    map_low = slot_map.astype(jnp.bfloat16)
    gate_rows = gate_here.reshape(2, half_cap)
    both = jnp.concatenate([tokens_in, out_grad], axis=1)
    send_xg = jnp.einsum(
        "erl,ld->erd", picked_low, both, preferred_element_type=jnp.float32
    ).astype(jnp.bfloat16)
    send_xg = send_xg.reshape(owners, 2 * width)
    recv_xg = lax.all_to_all(send_xg, "expert", split_axis=0, concat_axis=0, tiled=True)
    map_mine = lax.dynamic_index_in_dim(map_low, parity, 0, keepdims=False)
    rows_mine = jnp.dot(map_mine, recv_xg, preferred_element_type=jnp.float32).astype(
        jnp.bfloat16
    )
    rows_other = partner(rows_mine, "expert", 0)
    gate_mine = lax.dynamic_index_in_dim(gate_rows, parity, 0, keepdims=False)
    gate_other = lax.dynamic_index_in_dim(gate_rows, 1 - parity, 0, keepdims=False)
    rows_xg = jnp.stack([rows_mine, rows_other])
    gate_ord = jnp.stack([gate_mine, gate_other])
    gate_col = jnp.pad(gate_ord[:, :, None], ((0, 0), (0, 0), (0, 127)))
    packed = jnp.concatenate([rows_xg, gate_col], axis=2)
    all_p = lax.all_gather(packed, "dp", axis=1, tiled=True)
    flat_x = all_p[:, :, :width].reshape(-1, width)
    flat_g = all_p[:, :, width : 2 * width].reshape(-1, width)
    flat_gate = all_p[:, :, 2 * width].reshape(-1).astype(jnp.float32)
    up_part = w_up[0]
    down_part = w_down[0]
    pre_act = jnp.dot(flat_x, up_part, preferred_element_type=jnp.float32)
    act_value, act_slope = gelu_pair(pre_act)
    hidden = act_value.astype(jnp.bfloat16)
    back_grad = lax.dot_general(
        flat_g, down_part, (((1,), (1,)), ((), ())), preferred_element_type=jnp.float32
    )
    gate_terms = jnp.sum(hidden.astype(jnp.float32) * back_grad, axis=1)
    scaled = (flat_gate[:, None] * flat_g.astype(jnp.float32)).astype(jnp.bfloat16)
    pre_grad = (flat_gate[:, None] * back_grad * act_slope).astype(jnp.bfloat16)
    grad_down = lax.dot_general(
        hidden, scaled, (((0,), (0,)), ((), ())), preferred_element_type=jnp.float32
    )
    grad_up = lax.dot_general(
        flat_x, pre_grad, (((0,), (0,)), ((), ())), preferred_element_type=jnp.float32
    )
    dx_terms = lax.dot_general(
        pre_grad, up_part, (((1,), (1,)), ((), ())), preferred_element_type=jnp.float32
    )
    dx_low = dx_terms.reshape(2, groups * half_cap, width).astype(jnp.bfloat16)
    gate_low = gate_terms.reshape(2, groups * half_cap, 1).astype(jnp.bfloat16)
    gate_low = jnp.pad(gate_low, ((0, 0), (0, 0), (0, 127)))
    reduced = lax.psum_scatter(
        jnp.concatenate([dx_low, gate_low], axis=2),
        "dp",
        scatter_dimension=1,
        tiled=True,
    )
    from_partner = partner(reduced[1], "expert", 0)
    total = reduced[0].astype(jnp.float32) + from_partner.astype(jnp.float32)
    map_f32 = lax.dynamic_index_in_dim(slot_map, parity, 0, keepdims=False)
    spread = jnp.einsum("ij,id->jd", map_f32, total[:, :width], precision=highest)
    returned = lax.all_to_all(
        spread.astype(jnp.bfloat16), "expert", split_axis=0, concat_axis=0, tiled=True
    ).astype(jnp.float32)
    take_back = picked.reshape(owners, tok_local)
    in_grad = jnp.einsum("kl,kd->ld", take_back, returned, precision=highest)
    gate_out = total[:, width].reshape(1, 1, half_cap)
    return (
        in_grad.astype(jnp.bfloat16),
        grad_up.astype(jnp.bfloat16)[None],
        grad_down.astype(jnp.bfloat16)[None],
        gate_out,
    )


def solution(mesh):
    placed = (
        P(("dp", "expert"), None),
        P(("dp", "expert"), None),
        P("dp", None, None),
        P("dp", None),
        P("dp", None, None),
        P("expert", None, "dp"),
        P("expert", "dp", None),
    )
    return jax.shard_map(
        on_device,
        mesh=mesh,
        in_specs=placed,
        out_specs=(
            P(("dp", "expert"), None),
            P("expert", None, "dp"),
            P("expert", "dp", None),
            P("dp", "expert", None),
        ),
        check_vma=False,
    )
```

```python
import jax
import jax.numpy as jnp
from jax import lax
from jax.sharding import PartitionSpec as P

root_two_over_pi = 0.7978845608028654
cubic_coef = 0.044715


def partner(x, axis, apart):
    return lax.ppermute(x, axis, [(i, i ^ 1 << apart) for i in range(lax.axis_size(axis))])


def gelu_pair(pre_act):
    inner_arg = root_two_over_pi * (pre_act + cubic_coef * pre_act * pre_act * pre_act)
    tangent = jnp.tanh(inner_arg)
    act_value = 0.5 * pre_act * (1.0 + tangent)
    act_slope = 0.5 * (1.0 + tangent) + 0.5 * pre_act * (
        1.0 - tangent * tangent
    ) * root_two_over_pi * (1.0 + 3.0 * cubic_coef * pre_act * pre_act)
    return (act_value, act_slope)


def on_device(tokens_in, out_grad, chosen, counts, gates, w_up, w_down):
    tok_local = tokens_in.shape[0]
    width = tokens_in.shape[1]
    owners = lax.axis_size("expert")
    groups = lax.axis_size("dp")
    capacity = chosen.shape[2]
    half_cap = capacity // 2
    num_experts = chosen.shape[1]
    device = lax.axis_index("expert")
    expert = device // 2
    parity = device % 2
    highest = lax.Precision.HIGHEST
    my_lists = chosen[0]
    slot_ids = jnp.arange(capacity, dtype=jnp.int32)
    is_valid = slot_ids[None, :] < counts[0][:, None]
    owner_of = my_lists // tok_local
    local_of = my_lists % tok_local
    mine = jnp.logical_and(owner_of == device, is_valid)
    local_ids = jnp.arange(tok_local, dtype=jnp.int32)
    hits = jnp.logical_and(mine[:, :, None], local_of[:, :, None] == local_ids[None, None, :])
    picked = jnp.sum(hits.astype(jnp.float32).reshape(num_experts, 2, half_cap, tok_local), axis=2)
    picked_low = picked.astype(jnp.bfloat16)
    list_row = lax.dynamic_index_in_dim(my_lists, expert, 0, keepdims=False)
    count_here = lax.dynamic_index_in_dim(counts[0], expert, 0, keepdims=False)
    valid_here = slot_ids < count_here
    gate_here = jnp.where(
        valid_here,
        lax.dynamic_index_in_dim(gates[0], expert, 0, keepdims=False),
        jnp.zeros((), jnp.bfloat16),
    )
    owner_ids = jnp.arange(owners, dtype=jnp.int32)
    slot_map = jnp.logical_and(
        (list_row // tok_local)[:, None] == owner_ids[None, :], valid_here[:, None]
    )
    slot_map = slot_map.astype(jnp.float32).reshape(2, half_cap, owners)
    map_low = slot_map.astype(jnp.bfloat16)
    gate_rows = gate_here.reshape(2, half_cap)
    both = jnp.stack([tokens_in, out_grad])
    send_xg = jnp.einsum(
        "erl,sld->ersd", picked_low, both, preferred_element_type=jnp.float32
    ).astype(jnp.bfloat16)
    send_xg = send_xg.reshape(owners, 2, width)
    recv_xg = lax.all_to_all(send_xg, "expert", split_axis=0, concat_axis=0, tiled=True)
    map_mine = lax.dynamic_index_in_dim(map_low, parity, 0, keepdims=False)
    rows_mine = jnp.einsum(
        "ij,jsd->isd", map_mine, recv_xg, preferred_element_type=jnp.float32
    ).astype(jnp.bfloat16)
    rows_mine = rows_mine.reshape(half_cap, 2 * width)
    rows_other = partner(rows_mine, "expert", 0)
    gate_mine = lax.dynamic_index_in_dim(gate_rows, parity, 0, keepdims=False)
    gate_other = lax.dynamic_index_in_dim(gate_rows, 1 - parity, 0, keepdims=False)
    rows_xg = jnp.stack([rows_mine, rows_other])
    gate_ord = jnp.stack([gate_mine, gate_other])
    gate_col = jnp.pad(gate_ord[:, :, None], ((0, 0), (0, 0), (0, 127)))
    packed = jnp.concatenate([rows_xg, gate_col], axis=2)
    all_p = lax.all_gather(packed, "dp", axis=1, tiled=True)
    flat_x = all_p[:, :, :width].reshape(-1, width)
    flat_g = all_p[:, :, width : 2 * width].reshape(-1, width)
    flat_gate = all_p[:, :, 2 * width].reshape(-1).astype(jnp.float32)
    up_part = w_up[0]
    down_part = w_down[0]
    pre_act = jnp.dot(flat_x, up_part, preferred_element_type=jnp.float32)
    act_value, act_slope = gelu_pair(pre_act)
    hidden = act_value.astype(jnp.bfloat16)
    back_grad = lax.dot_general(
        flat_g, down_part, (((1,), (1,)), ((), ())), preferred_element_type=jnp.float32
    )
    gate_terms = jnp.sum(hidden.astype(jnp.float32) * back_grad, axis=1)
    scaled = (flat_gate[:, None] * flat_g.astype(jnp.float32)).astype(jnp.bfloat16)
    pre_grad = (flat_gate[:, None] * back_grad * act_slope).astype(jnp.bfloat16)
    grad_down = lax.dot_general(
        hidden, scaled, (((0,), (0,)), ((), ())), preferred_element_type=jnp.float32
    )
    grad_up = lax.dot_general(
        flat_x, pre_grad, (((0,), (0,)), ((), ())), preferred_element_type=jnp.float32
    )
    dx_terms = lax.dot_general(
        pre_grad, up_part, (((1,), (1,)), ((), ())), preferred_element_type=jnp.float32
    )
    dx_low = dx_terms.reshape(2, groups * half_cap, width).astype(jnp.bfloat16)
    gate_low = gate_terms.reshape(2, groups * half_cap, 1).astype(jnp.bfloat16)
    gate_low = jnp.pad(gate_low, ((0, 0), (0, 0), (0, 127)))
    reduced = lax.psum_scatter(
        jnp.concatenate([dx_low, gate_low], axis=2),
        "dp",
        scatter_dimension=1,
        tiled=True,
    )
    from_partner = partner(reduced[1], "expert", 0)
    total = reduced[0].astype(jnp.float32) + from_partner.astype(jnp.float32)
    map_f32 = lax.dynamic_index_in_dim(slot_map, parity, 0, keepdims=False)
    dx_total = total[:, :width].reshape(half_cap, 2, width // 2)
    spread = jnp.einsum("ij,isd->jsd", map_f32, dx_total, precision=highest)
    returned = lax.all_to_all(
        spread.astype(jnp.bfloat16), "expert", split_axis=0, concat_axis=0, tiled=True
    ).astype(jnp.float32)
    take_back = picked.reshape(owners, tok_local)
    in_grad = jnp.einsum("kl,ksd->lsd", take_back, returned, precision=highest)
    in_grad = in_grad.reshape(tok_local, width)
    gate_out = total[:, width].reshape(1, 1, half_cap)
    return (
        in_grad.astype(jnp.bfloat16),
        grad_up.astype(jnp.bfloat16)[None],
        grad_down.astype(jnp.bfloat16)[None],
        gate_out,
    )


def solution(mesh):
    placed = (
        P(("dp", "expert"), None),
        P(("dp", "expert"), None),
        P("dp", None, None),
        P("dp", None),
        P("dp", None, None),
        P("expert", None, "dp"),
        P("expert", "dp", None),
    )
    return jax.shard_map(
        on_device,
        mesh=mesh,
        in_specs=placed,
        out_specs=(
            P(("dp", "expert"), None),
            P("expert", None, "dp"),
            P("expert", "dp", None),
            P("dp", "expert", None),
        ),
        check_vma=False,
    )
```

```python
import jax
import jax.numpy as jnp
from jax import lax
from jax.sharding import PartitionSpec as P

root_two_over_pi = 0.7978845608028654
cubic_coef = 0.044715


def partner(x, axis, apart):
    return lax.ppermute(x, axis, [(i, i ^ 1 << apart) for i in range(lax.axis_size(axis))])


def dp_shift(x, step, groups):
    chips = groups // 2
    pairs = [(i, ((i // 2 + step) % chips) * 2 + i % 2) for i in range(groups)]
    return lax.ppermute(x, "dp", pairs)


def dp_reduce_scatter(terms, groups):
    chips = groups // 2
    me = lax.axis_index("dp")
    chip = me // 2
    core = me % 2
    split = terms.reshape(terms.shape[0], chips, 2, -1, terms.shape[2])
    keep = lax.dynamic_index_in_dim(split, core, 2, keepdims=False)
    give = lax.dynamic_index_in_dim(split, 1 - core, 2, keepdims=False)
    got = partner(give, "dp", 0)
    pair_sum = keep.astype(jnp.float32) + got.astype(jnp.float32)
    pair_low = pair_sum.astype(jnp.bfloat16)
    total = lax.dynamic_index_in_dim(pair_sum, chip, 1, keepdims=False)
    for step in range(1, chips):
        piece = lax.dynamic_index_in_dim(pair_low, (chip + step) % chips, 1, keepdims=False)
        total = total + dp_shift(piece, step, groups).astype(jnp.float32)
    return total


def gelu_pair(pre_act):
    inner_arg = root_two_over_pi * (pre_act + cubic_coef * pre_act * pre_act * pre_act)
    tangent = jnp.tanh(inner_arg)
    act_value = 0.5 * pre_act * (1.0 + tangent)
    act_slope = 0.5 * (1.0 + tangent) + 0.5 * pre_act * (
        1.0 - tangent * tangent
    ) * root_two_over_pi * (1.0 + 3.0 * cubic_coef * pre_act * pre_act)
    return (act_value, act_slope)


def on_device(tokens_in, out_grad, chosen, counts, gates, w_up, w_down):
    tok_local = tokens_in.shape[0]
    width = tokens_in.shape[1]
    owners = lax.axis_size("expert")
    groups = lax.axis_size("dp")
    capacity = chosen.shape[2]
    half_cap = capacity // 2
    num_experts = chosen.shape[1]
    device = lax.axis_index("expert")
    expert = device // 2
    parity = device % 2
    highest = lax.Precision.HIGHEST
    my_lists = chosen[0]
    slot_ids = jnp.arange(capacity, dtype=jnp.int32)
    is_valid = slot_ids[None, :] < counts[0][:, None]
    owner_of = my_lists // tok_local
    local_of = my_lists % tok_local
    mine = jnp.logical_and(owner_of == device, is_valid)
    local_ids = jnp.arange(tok_local, dtype=jnp.int32)
    hits = jnp.logical_and(mine[:, :, None], local_of[:, :, None] == local_ids[None, None, :])
    picked = jnp.sum(hits.astype(jnp.float32).reshape(num_experts, 2, half_cap, tok_local), axis=2)
    picked_low = picked.astype(jnp.bfloat16)
    list_row = lax.dynamic_index_in_dim(my_lists, expert, 0, keepdims=False)
    count_here = lax.dynamic_index_in_dim(counts[0], expert, 0, keepdims=False)
    valid_here = slot_ids < count_here
    gate_here = jnp.where(
        valid_here,
        lax.dynamic_index_in_dim(gates[0], expert, 0, keepdims=False),
        jnp.zeros((), jnp.bfloat16),
    )
    owner_ids = jnp.arange(owners, dtype=jnp.int32)
    slot_map = jnp.logical_and(
        (list_row // tok_local)[:, None] == owner_ids[None, :], valid_here[:, None]
    )
    slot_map = slot_map.astype(jnp.float32).reshape(2, half_cap, owners)
    map_low = slot_map.astype(jnp.bfloat16)
    gate_rows = gate_here.reshape(2, half_cap)
    both = jnp.stack([tokens_in, out_grad])
    send_xg = jnp.einsum(
        "erl,sld->ersd", picked_low, both, preferred_element_type=jnp.float32
    ).astype(jnp.bfloat16)
    send_xg = send_xg.reshape(owners, 2, width)
    recv_xg = lax.all_to_all(send_xg, "expert", split_axis=0, concat_axis=0, tiled=True)
    map_mine = lax.dynamic_index_in_dim(map_low, parity, 0, keepdims=False)
    rows_mine = jnp.einsum(
        "ij,jsd->isd", map_mine, recv_xg, preferred_element_type=jnp.float32
    ).astype(jnp.bfloat16)
    rows_mine = rows_mine.reshape(half_cap, 2 * width)
    rows_other = partner(rows_mine, "expert", 0)
    gate_mine = lax.dynamic_index_in_dim(gate_rows, parity, 0, keepdims=False)
    gate_other = lax.dynamic_index_in_dim(gate_rows, 1 - parity, 0, keepdims=False)
    rows_xg = jnp.stack([rows_mine, rows_other])
    gate_ord = jnp.stack([gate_mine, gate_other])
    gate_col = jnp.pad(gate_ord[:, :, None], ((0, 0), (0, 0), (0, 127)))
    packed = jnp.concatenate([rows_xg, gate_col], axis=2)
    all_p = lax.all_gather(packed, "dp", axis=1, tiled=True)
    flat_x = all_p[:, :, :width].reshape(-1, width)
    flat_g = all_p[:, :, width : 2 * width].reshape(-1, width)
    flat_gate = all_p[:, :, 2 * width].reshape(-1).astype(jnp.float32)
    up_part = w_up[0]
    down_part = w_down[0]
    pre_act = jnp.dot(flat_x, up_part, preferred_element_type=jnp.float32)
    act_value, act_slope = gelu_pair(pre_act)
    hidden = act_value.astype(jnp.bfloat16)
    back_grad = lax.dot_general(
        flat_g, down_part, (((1,), (1,)), ((), ())), preferred_element_type=jnp.float32
    )
    gate_terms = jnp.sum(hidden.astype(jnp.float32) * back_grad, axis=1)
    scaled = (flat_gate[:, None] * flat_g.astype(jnp.float32)).astype(jnp.bfloat16)
    pre_grad = (flat_gate[:, None] * back_grad * act_slope).astype(jnp.bfloat16)
    grad_down = lax.dot_general(
        hidden, scaled, (((0,), (0,)), ((), ())), preferred_element_type=jnp.float32
    )
    grad_up = lax.dot_general(
        flat_x, pre_grad, (((0,), (0,)), ((), ())), preferred_element_type=jnp.float32
    )
    dx_terms = lax.dot_general(
        pre_grad, up_part, (((1,), (1,)), ((), ())), preferred_element_type=jnp.float32
    )
    dx_low = dx_terms.reshape(2, groups * half_cap, width).astype(jnp.bfloat16)
    gate_low = gate_terms.reshape(2, groups * half_cap, 1).astype(jnp.bfloat16)
    gate_low = jnp.pad(gate_low, ((0, 0), (0, 0), (0, 127)))
    reduced = dp_reduce_scatter(jnp.concatenate([dx_low, gate_low], axis=2), groups)
    reduced_low = reduced.astype(jnp.bfloat16)
    from_partner = partner(reduced_low[1], "expert", 0)
    total = reduced[0] + from_partner.astype(jnp.float32)
    map_f32 = lax.dynamic_index_in_dim(slot_map, parity, 0, keepdims=False)
    dx_total = total[:, :width].reshape(half_cap, 2, width // 2)
    spread = jnp.einsum("ij,isd->jsd", map_f32, dx_total, precision=highest)
    returned = lax.all_to_all(
        spread.astype(jnp.bfloat16), "expert", split_axis=0, concat_axis=0, tiled=True
    ).astype(jnp.float32)
    take_back = picked.reshape(owners, tok_local)
    in_grad = jnp.einsum("kl,ksd->lsd", take_back, returned, precision=highest)
    in_grad = in_grad.reshape(tok_local, width)
    gate_out = total[:, width].reshape(1, 1, half_cap)
    return (
        in_grad.astype(jnp.bfloat16),
        grad_up.astype(jnp.bfloat16)[None],
        grad_down.astype(jnp.bfloat16)[None],
        gate_out,
    )


def solution(mesh):
    placed = (
        P(("dp", "expert"), None),
        P(("dp", "expert"), None),
        P("dp", None, None),
        P("dp", None),
        P("dp", None, None),
        P("expert", None, "dp"),
        P("expert", "dp", None),
    )
    return jax.shard_map(
        on_device,
        mesh=mesh,
        in_specs=placed,
        out_specs=(
            P(("dp", "expert"), None),
            P("expert", None, "dp"),
            P("expert", "dp", None),
            P("dp", "expert", None),
        ),
        check_vma=False,
    )
```

```python
import jax
import jax.numpy as jnp
from jax import lax
from jax.sharding import PartitionSpec as P

root_two_over_pi = 0.7978845608028654
cubic_coef = 0.044715


def partner(x, axis, apart):
    return lax.ppermute(x, axis, [(i, i ^ 1 << apart) for i in range(lax.axis_size(axis))])


def dp_shift(x, step, groups):
    chips = groups // 2
    pairs = [(i, ((i // 2 + step) % chips) * 2 + i % 2) for i in range(groups)]
    return lax.ppermute(x, "dp", pairs)


def dp_reduce_scatter(terms, groups):
    chips = groups // 2
    me = lax.axis_index("dp")
    chip = me // 2
    core = me % 2
    split = terms.reshape(terms.shape[0], chips, 2, -1, terms.shape[2])
    keep = lax.dynamic_index_in_dim(split, core, 2, keepdims=False)
    give = lax.dynamic_index_in_dim(split, 1 - core, 2, keepdims=False)
    got = partner(give, "dp", 0)
    pair_sum = keep.astype(jnp.float32) + got.astype(jnp.float32)
    from_pair = partner(pair_sum[1].astype(jnp.bfloat16), "expert", 0)
    half_sum = pair_sum[0] + from_pair.astype(jnp.float32)
    half_low = half_sum.astype(jnp.bfloat16)
    total = lax.dynamic_index_in_dim(half_sum, chip, 0, keepdims=False)
    for step in range(1, chips):
        piece = lax.dynamic_index_in_dim(half_low, (chip + step) % chips, 0, keepdims=False)
        total = total + dp_shift(piece, step, groups).astype(jnp.float32)
    return total


def gelu_pair(pre_act):
    inner_arg = root_two_over_pi * (pre_act + cubic_coef * pre_act * pre_act * pre_act)
    tangent = jnp.tanh(inner_arg)
    act_value = 0.5 * pre_act * (1.0 + tangent)
    act_slope = 0.5 * (1.0 + tangent) + 0.5 * pre_act * (
        1.0 - tangent * tangent
    ) * root_two_over_pi * (1.0 + 3.0 * cubic_coef * pre_act * pre_act)
    return (act_value, act_slope)


def on_device(tokens_in, out_grad, chosen, counts, gates, w_up, w_down):
    tok_local = tokens_in.shape[0]
    width = tokens_in.shape[1]
    owners = lax.axis_size("expert")
    groups = lax.axis_size("dp")
    capacity = chosen.shape[2]
    half_cap = capacity // 2
    num_experts = chosen.shape[1]
    device = lax.axis_index("expert")
    expert = device // 2
    parity = device % 2
    highest = lax.Precision.HIGHEST
    my_lists = chosen[0]
    slot_ids = jnp.arange(capacity, dtype=jnp.int32)
    is_valid = slot_ids[None, :] < counts[0][:, None]
    owner_of = my_lists // tok_local
    local_of = my_lists % tok_local
    mine = jnp.logical_and(owner_of == device, is_valid)
    local_ids = jnp.arange(tok_local, dtype=jnp.int32)
    hits = jnp.logical_and(mine[:, :, None], local_of[:, :, None] == local_ids[None, None, :])
    picked = jnp.sum(hits.astype(jnp.float32).reshape(num_experts, 2, half_cap, tok_local), axis=2)
    picked_low = picked.astype(jnp.bfloat16)
    list_row = lax.dynamic_index_in_dim(my_lists, expert, 0, keepdims=False)
    count_here = lax.dynamic_index_in_dim(counts[0], expert, 0, keepdims=False)
    valid_here = slot_ids < count_here
    gate_here = jnp.where(
        valid_here,
        lax.dynamic_index_in_dim(gates[0], expert, 0, keepdims=False),
        jnp.zeros((), jnp.bfloat16),
    )
    owner_ids = jnp.arange(owners, dtype=jnp.int32)
    slot_map = jnp.logical_and(
        (list_row // tok_local)[:, None] == owner_ids[None, :], valid_here[:, None]
    )
    slot_map = slot_map.astype(jnp.float32).reshape(2, half_cap, owners)
    map_low = slot_map.astype(jnp.bfloat16)
    gate_rows = gate_here.reshape(2, half_cap)
    both = jnp.stack([tokens_in, out_grad])
    send_xg = jnp.einsum(
        "erl,sld->ersd", picked_low, both, preferred_element_type=jnp.float32
    ).astype(jnp.bfloat16)
    send_xg = send_xg.reshape(owners, 2, width)
    recv_xg = lax.all_to_all(send_xg, "expert", split_axis=0, concat_axis=0, tiled=True)
    map_mine = lax.dynamic_index_in_dim(map_low, parity, 0, keepdims=False)
    rows_mine = jnp.einsum(
        "ij,jsd->isd", map_mine, recv_xg, preferred_element_type=jnp.float32
    ).astype(jnp.bfloat16)
    rows_mine = rows_mine.reshape(half_cap, 2 * width)
    rows_other = partner(rows_mine, "expert", 0)
    gate_mine = lax.dynamic_index_in_dim(gate_rows, parity, 0, keepdims=False)
    gate_other = lax.dynamic_index_in_dim(gate_rows, 1 - parity, 0, keepdims=False)
    rows_xg = jnp.stack([rows_mine, rows_other])
    gate_ord = jnp.stack([gate_mine, gate_other])
    gate_col = jnp.pad(gate_ord[:, :, None], ((0, 0), (0, 0), (0, 127)))
    packed = jnp.concatenate([rows_xg, gate_col], axis=2)
    all_p = lax.all_gather(packed, "dp", axis=1, tiled=True)
    flat_x = all_p[:, :, :width].reshape(-1, width)
    flat_g = all_p[:, :, width : 2 * width].reshape(-1, width)
    flat_gate = all_p[:, :, 2 * width].reshape(-1).astype(jnp.float32)
    up_part = w_up[0]
    down_part = w_down[0]
    pre_act = jnp.dot(flat_x, up_part, preferred_element_type=jnp.float32)
    act_value, act_slope = gelu_pair(pre_act)
    hidden = act_value.astype(jnp.bfloat16)
    back_grad = lax.dot_general(
        flat_g, down_part, (((1,), (1,)), ((), ())), preferred_element_type=jnp.float32
    )
    gate_terms = jnp.sum(hidden.astype(jnp.float32) * back_grad, axis=1)
    scaled = (flat_gate[:, None] * flat_g.astype(jnp.float32)).astype(jnp.bfloat16)
    pre_grad = (flat_gate[:, None] * back_grad * act_slope).astype(jnp.bfloat16)
    grad_down = lax.dot_general(
        hidden, scaled, (((0,), (0,)), ((), ())), preferred_element_type=jnp.float32
    )
    grad_up = lax.dot_general(
        flat_x, pre_grad, (((0,), (0,)), ((), ())), preferred_element_type=jnp.float32
    )
    dx_terms = lax.dot_general(
        pre_grad, up_part, (((1,), (1,)), ((), ())), preferred_element_type=jnp.float32
    )
    dx_low = dx_terms.reshape(2, groups * half_cap, width).astype(jnp.bfloat16)
    gate_low = gate_terms.reshape(2, groups * half_cap, 1).astype(jnp.bfloat16)
    gate_low = jnp.pad(gate_low, ((0, 0), (0, 0), (0, 127)))
    reduced = dp_reduce_scatter(jnp.concatenate([dx_low, gate_low], axis=2), groups)
    total = reduced
    map_f32 = lax.dynamic_index_in_dim(slot_map, parity, 0, keepdims=False)
    dx_total = total[:, :width].reshape(half_cap, 2, width // 2)
    spread = jnp.einsum("ij,isd->jsd", map_f32, dx_total, precision=highest)
    returned = lax.all_to_all(
        spread.astype(jnp.bfloat16), "expert", split_axis=0, concat_axis=0, tiled=True
    ).astype(jnp.float32)
    take_back = picked.reshape(owners, tok_local)
    in_grad = jnp.einsum("kl,ksd->lsd", take_back, returned, precision=highest)
    in_grad = in_grad.reshape(tok_local, width)
    gate_out = total[:, width].reshape(1, 1, half_cap)
    return (
        in_grad.astype(jnp.bfloat16),
        grad_up.astype(jnp.bfloat16)[None],
        grad_down.astype(jnp.bfloat16)[None],
        gate_out,
    )


def solution(mesh):
    placed = (
        P(("dp", "expert"), None),
        P(("dp", "expert"), None),
        P("dp", None, None),
        P("dp", None),
        P("dp", None, None),
        P("expert", None, "dp"),
        P("expert", "dp", None),
    )
    return jax.shard_map(
        on_device,
        mesh=mesh,
        in_specs=placed,
        out_specs=(
            P(("dp", "expert"), None),
            P("expert", None, "dp"),
            P("expert", "dp", None),
            P("dp", "expert", None),
        ),
        check_vma=False,
    )
```

```python
import jax
import jax.numpy as jnp
from jax import lax
from jax.sharding import PartitionSpec as P

root_two_over_pi = 0.7978845608028654
cubic_coef = 0.044715


def partner(x, axis, apart):
    return lax.ppermute(x, axis, [(i, i ^ 1 << apart) for i in range(lax.axis_size(axis))])


def dp_shift(x, step, groups):
    chips = groups // 2
    pairs = [(i, ((i // 2 + step) % chips) * 2 + i % 2) for i in range(groups)]
    return lax.ppermute(x, "dp", pairs)


def dp_all_gather(block, groups):
    chips = groups // 2
    me = lax.axis_index("dp")
    chip = me // 2
    core = me % 2
    by_step = jnp.stack([block] + [dp_shift(block, step, groups) for step in range(1, chips)])
    mine = jnp.stack(
        [
            lax.dynamic_index_in_dim(by_step, (chip - place) % chips, 0, keepdims=False)
            for place in range(chips)
        ]
    )
    theirs = partner(mine, "dp", 0)
    both_cores = jnp.stack([mine, theirs])
    first = lax.dynamic_index_in_dim(both_cores, core, 0, keepdims=False)
    second = lax.dynamic_index_in_dim(both_cores, 1 - core, 0, keepdims=False)
    full = jnp.stack([first, second], axis=1)
    full = jnp.moveaxis(full, 2, 0)
    return full.reshape(block.shape[0], groups * block.shape[1], block.shape[2])


def dp_reduce_scatter(terms, groups):
    chips = groups // 2
    me = lax.axis_index("dp")
    chip = me // 2
    core = me % 2
    split = terms.reshape(terms.shape[0], chips, 2, -1, terms.shape[2])
    keep = lax.dynamic_index_in_dim(split, core, 2, keepdims=False)
    give = lax.dynamic_index_in_dim(split, 1 - core, 2, keepdims=False)
    got = partner(give, "dp", 0)
    pair_sum = keep.astype(jnp.float32) + got.astype(jnp.float32)
    pair_low = pair_sum.astype(jnp.bfloat16)
    total = lax.dynamic_index_in_dim(pair_sum, chip, 1, keepdims=False)
    for step in range(1, chips):
        piece = lax.dynamic_index_in_dim(pair_low, (chip + step) % chips, 1, keepdims=False)
        total = total + dp_shift(piece, step, groups).astype(jnp.float32)
    return total


def gelu_pair(pre_act):
    inner_arg = root_two_over_pi * (pre_act + cubic_coef * pre_act * pre_act * pre_act)
    tangent = jnp.tanh(inner_arg)
    act_value = 0.5 * pre_act * (1.0 + tangent)
    act_slope = 0.5 * (1.0 + tangent) + 0.5 * pre_act * (
        1.0 - tangent * tangent
    ) * root_two_over_pi * (1.0 + 3.0 * cubic_coef * pre_act * pre_act)
    return (act_value, act_slope)


def on_device(tokens_in, out_grad, chosen, counts, gates, w_up, w_down):
    tok_local = tokens_in.shape[0]
    width = tokens_in.shape[1]
    owners = lax.axis_size("expert")
    groups = lax.axis_size("dp")
    capacity = chosen.shape[2]
    half_cap = capacity // 2
    num_experts = chosen.shape[1]
    device = lax.axis_index("expert")
    expert = device // 2
    parity = device % 2
    highest = lax.Precision.HIGHEST
    my_lists = chosen[0]
    slot_ids = jnp.arange(capacity, dtype=jnp.int32)
    is_valid = slot_ids[None, :] < counts[0][:, None]
    owner_of = my_lists // tok_local
    local_of = my_lists % tok_local
    mine = jnp.logical_and(owner_of == device, is_valid)
    local_ids = jnp.arange(tok_local, dtype=jnp.int32)
    hits = jnp.logical_and(mine[:, :, None], local_of[:, :, None] == local_ids[None, None, :])
    picked = jnp.sum(hits.astype(jnp.float32).reshape(num_experts, 2, half_cap, tok_local), axis=2)
    picked_low = picked.astype(jnp.bfloat16)
    list_row = lax.dynamic_index_in_dim(my_lists, expert, 0, keepdims=False)
    count_here = lax.dynamic_index_in_dim(counts[0], expert, 0, keepdims=False)
    valid_here = slot_ids < count_here
    gate_here = jnp.where(
        valid_here,
        lax.dynamic_index_in_dim(gates[0], expert, 0, keepdims=False),
        jnp.zeros((), jnp.bfloat16),
    )
    owner_ids = jnp.arange(owners, dtype=jnp.int32)
    slot_map = jnp.logical_and(
        (list_row // tok_local)[:, None] == owner_ids[None, :], valid_here[:, None]
    )
    slot_map = slot_map.astype(jnp.float32).reshape(2, half_cap, owners)
    map_low = slot_map.astype(jnp.bfloat16)
    gate_rows = gate_here.reshape(2, half_cap)
    both = jnp.stack([tokens_in, out_grad])
    send_xg = jnp.einsum(
        "erl,sld->ersd", picked_low, both, preferred_element_type=jnp.float32
    ).astype(jnp.bfloat16)
    send_xg = send_xg.reshape(owners, 2, width)
    recv_xg = lax.all_to_all(send_xg, "expert", split_axis=0, concat_axis=0, tiled=True)
    map_mine = lax.dynamic_index_in_dim(map_low, parity, 0, keepdims=False)
    rows_mine = jnp.einsum(
        "ij,jsd->isd", map_mine, recv_xg, preferred_element_type=jnp.float32
    ).astype(jnp.bfloat16)
    rows_mine = rows_mine.reshape(half_cap, 2 * width)
    rows_other = partner(rows_mine, "expert", 0)
    gate_mine = lax.dynamic_index_in_dim(gate_rows, parity, 0, keepdims=False)
    gate_other = lax.dynamic_index_in_dim(gate_rows, 1 - parity, 0, keepdims=False)
    rows_xg = jnp.stack([rows_mine, rows_other])
    gate_ord = jnp.stack([gate_mine, gate_other])
    gate_col = jnp.pad(gate_ord[:, :, None], ((0, 0), (0, 0), (0, 127)))
    packed = jnp.concatenate([rows_xg, gate_col], axis=2)
    all_p = dp_all_gather(packed, groups)
    flat_x = all_p[:, :, :width].reshape(-1, width)
    flat_g = all_p[:, :, width : 2 * width].reshape(-1, width)
    flat_gate = all_p[:, :, 2 * width].reshape(-1).astype(jnp.float32)
    up_part = w_up[0]
    down_part = w_down[0]
    pre_act = jnp.dot(flat_x, up_part, preferred_element_type=jnp.float32)
    act_value, act_slope = gelu_pair(pre_act)
    hidden = act_value.astype(jnp.bfloat16)
    back_grad = lax.dot_general(
        flat_g, down_part, (((1,), (1,)), ((), ())), preferred_element_type=jnp.float32
    )
    gate_terms = jnp.sum(hidden.astype(jnp.float32) * back_grad, axis=1)
    scaled = (flat_gate[:, None] * flat_g.astype(jnp.float32)).astype(jnp.bfloat16)
    pre_grad = (flat_gate[:, None] * back_grad * act_slope).astype(jnp.bfloat16)
    grad_down = lax.dot_general(
        hidden, scaled, (((0,), (0,)), ((), ())), preferred_element_type=jnp.float32
    )
    grad_up = lax.dot_general(
        flat_x, pre_grad, (((0,), (0,)), ((), ())), preferred_element_type=jnp.float32
    )
    dx_terms = lax.dot_general(
        pre_grad, up_part, (((1,), (1,)), ((), ())), preferred_element_type=jnp.float32
    )
    dx_low = dx_terms.reshape(2, groups * half_cap, width).astype(jnp.bfloat16)
    gate_low = gate_terms.reshape(2, groups * half_cap, 1).astype(jnp.bfloat16)
    gate_low = jnp.pad(gate_low, ((0, 0), (0, 0), (0, 127)))
    reduced = dp_reduce_scatter(jnp.concatenate([dx_low, gate_low], axis=2), groups)
    reduced_low = reduced.astype(jnp.bfloat16)
    from_partner = partner(reduced_low[1], "expert", 0)
    total = reduced[0] + from_partner.astype(jnp.float32)
    map_f32 = lax.dynamic_index_in_dim(slot_map, parity, 0, keepdims=False)
    dx_total = total[:, :width].reshape(half_cap, 2, width // 2)
    spread = jnp.einsum("ij,isd->jsd", map_f32, dx_total, precision=highest)
    returned = lax.all_to_all(
        spread.astype(jnp.bfloat16), "expert", split_axis=0, concat_axis=0, tiled=True
    ).astype(jnp.float32)
    take_back = picked.reshape(owners, tok_local)
    in_grad = jnp.einsum("kl,ksd->lsd", take_back, returned, precision=highest)
    in_grad = in_grad.reshape(tok_local, width)
    gate_out = total[:, width].reshape(1, 1, half_cap)
    return (
        in_grad.astype(jnp.bfloat16),
        grad_up.astype(jnp.bfloat16)[None],
        grad_down.astype(jnp.bfloat16)[None],
        gate_out,
    )


def solution(mesh):
    placed = (
        P(("dp", "expert"), None),
        P(("dp", "expert"), None),
        P("dp", None, None),
        P("dp", None),
        P("dp", None, None),
        P("expert", None, "dp"),
        P("expert", "dp", None),
    )
    return jax.shard_map(
        on_device,
        mesh=mesh,
        in_specs=placed,
        out_specs=(
            P(("dp", "expert"), None),
            P("expert", None, "dp"),
            P("expert", "dp", None),
            P("dp", "expert", None),
        ),
        check_vma=False,
    )
```

```python
import jax
import jax.numpy as jnp
from jax import lax
from jax.sharding import PartitionSpec as P

root_two_over_pi = 0.7978845608028654
cubic_coef = 0.044715


def partner(x, axis, apart):
    return lax.ppermute(x, axis, [(i, i ^ 1 << apart) for i in range(lax.axis_size(axis))])


def dp_shift(x, step, groups):
    chips = groups // 2
    pairs = [(i, ((i // 2 + step) % chips) * 2 + i % 2) for i in range(groups)]
    return lax.ppermute(x, "dp", pairs)


def dp_all_gather(block, groups):
    chips = groups // 2
    chip = lax.axis_index("dp") // 2
    by_step = jnp.stack([block] + [dp_shift(block, step, groups) for step in range(1, chips)])
    mine = jnp.stack(
        [
            lax.dynamic_index_in_dim(by_step, (chip - place) % chips, 0, keepdims=False)
            for place in range(chips)
        ]
    )
    return mine, partner(mine, "dp", 0)


def dp_reduce_scatter(keep, give, groups):
    chips = groups // 2
    chip = lax.axis_index("dp") // 2
    got = partner(give, "dp", 0)
    pair_sum = keep.astype(jnp.float32) + got.astype(jnp.float32)
    pair_low = pair_sum.astype(jnp.bfloat16)
    total = lax.dynamic_index_in_dim(pair_sum, chip, 0, keepdims=False)
    for step in range(1, chips):
        piece = lax.dynamic_index_in_dim(pair_low, (chip + step) % chips, 0, keepdims=False)
        total = total + dp_shift(piece, step, groups).astype(jnp.float32)
    return total


def expert_math(chunk, up_part, down_part):
    width = up_part.shape[0]
    rows = chunk.reshape(-1, chunk.shape[-1])
    flat_x = rows[:, :width]
    flat_g = rows[:, width : 2 * width]
    flat_gate = rows[:, 2 * width].astype(jnp.float32)
    pre_act = jnp.dot(flat_x, up_part, preferred_element_type=jnp.float32)
    act_value, act_slope = gelu_pair(pre_act)
    hidden = act_value.astype(jnp.bfloat16)
    back_grad = lax.dot_general(
        flat_g, down_part, (((1,), (1,)), ((), ())), preferred_element_type=jnp.float32
    )
    gate_terms = jnp.sum(hidden.astype(jnp.float32) * back_grad, axis=1)
    scaled = (flat_gate[:, None] * flat_g.astype(jnp.float32)).astype(jnp.bfloat16)
    pre_grad = (flat_gate[:, None] * back_grad * act_slope).astype(jnp.bfloat16)
    dx_terms = lax.dot_general(
        pre_grad, up_part, (((1,), (1,)), ((), ())), preferred_element_type=jnp.float32
    )
    dx_low = dx_terms.astype(jnp.bfloat16)
    gate_low = jnp.pad(gate_terms.astype(jnp.bfloat16)[:, None], ((0, 0), (0, 127)))
    terms = jnp.concatenate([dx_low, gate_low], axis=1)
    terms = terms.reshape(chunk.shape[:-1] + (terms.shape[-1],))
    grad_down = lax.dot_general(
        hidden, scaled, (((0,), (0,)), ((), ())), preferred_element_type=jnp.float32
    )
    grad_up = lax.dot_general(
        flat_x, pre_grad, (((0,), (0,)), ((), ())), preferred_element_type=jnp.float32
    )
    return terms, grad_up, grad_down


def gelu_pair(pre_act):
    inner_arg = root_two_over_pi * (pre_act + cubic_coef * pre_act * pre_act * pre_act)
    tangent = jnp.tanh(inner_arg)
    act_value = 0.5 * pre_act * (1.0 + tangent)
    act_slope = 0.5 * (1.0 + tangent) + 0.5 * pre_act * (
        1.0 - tangent * tangent
    ) * root_two_over_pi * (1.0 + 3.0 * cubic_coef * pre_act * pre_act)
    return (act_value, act_slope)


def on_device(tokens_in, out_grad, chosen, counts, gates, w_up, w_down):
    tok_local = tokens_in.shape[0]
    width = tokens_in.shape[1]
    owners = lax.axis_size("expert")
    groups = lax.axis_size("dp")
    capacity = chosen.shape[2]
    half_cap = capacity // 2
    num_experts = chosen.shape[1]
    device = lax.axis_index("expert")
    expert = device // 2
    parity = device % 2
    highest = lax.Precision.HIGHEST
    my_lists = chosen[0]
    slot_ids = jnp.arange(capacity, dtype=jnp.int32)
    is_valid = slot_ids[None, :] < counts[0][:, None]
    owner_of = my_lists // tok_local
    local_of = my_lists % tok_local
    mine = jnp.logical_and(owner_of == device, is_valid)
    local_ids = jnp.arange(tok_local, dtype=jnp.int32)
    hits = jnp.logical_and(mine[:, :, None], local_of[:, :, None] == local_ids[None, None, :])
    picked = jnp.sum(hits.astype(jnp.float32).reshape(num_experts, 2, half_cap, tok_local), axis=2)
    picked_low = picked.astype(jnp.bfloat16)
    list_row = lax.dynamic_index_in_dim(my_lists, expert, 0, keepdims=False)
    count_here = lax.dynamic_index_in_dim(counts[0], expert, 0, keepdims=False)
    valid_here = slot_ids < count_here
    gate_here = jnp.where(
        valid_here,
        lax.dynamic_index_in_dim(gates[0], expert, 0, keepdims=False),
        jnp.zeros((), jnp.bfloat16),
    )
    owner_ids = jnp.arange(owners, dtype=jnp.int32)
    slot_map = jnp.logical_and(
        (list_row // tok_local)[:, None] == owner_ids[None, :], valid_here[:, None]
    )
    slot_map = slot_map.astype(jnp.float32).reshape(2, half_cap, owners)
    map_low = slot_map.astype(jnp.bfloat16)
    gate_rows = gate_here.reshape(2, half_cap)
    both = jnp.stack([tokens_in, out_grad])
    send_xg = jnp.einsum(
        "erl,sld->ersd", picked_low, both, preferred_element_type=jnp.float32
    ).astype(jnp.bfloat16)
    send_xg = send_xg.reshape(owners, 2, width)
    recv_xg = lax.all_to_all(send_xg, "expert", split_axis=0, concat_axis=0, tiled=True)
    map_mine = lax.dynamic_index_in_dim(map_low, parity, 0, keepdims=False)
    rows_mine = jnp.einsum(
        "ij,jsd->isd", map_mine, recv_xg, preferred_element_type=jnp.float32
    ).astype(jnp.bfloat16)
    rows_mine = rows_mine.reshape(half_cap, 2 * width)
    rows_other = partner(rows_mine, "expert", 0)
    gate_mine = lax.dynamic_index_in_dim(gate_rows, parity, 0, keepdims=False)
    gate_other = lax.dynamic_index_in_dim(gate_rows, 1 - parity, 0, keepdims=False)
    rows_xg = jnp.stack([rows_mine, rows_other])
    gate_ord = jnp.stack([gate_mine, gate_other])
    gate_col = jnp.pad(gate_ord[:, :, None], ((0, 0), (0, 0), (0, 127)))
    packed = jnp.concatenate([rows_xg, gate_col], axis=2)
    mine_rows, their_rows = dp_all_gather(packed, groups)
    up_part = w_up[0]
    down_part = w_down[0]
    keep, up_mine, down_mine = expert_math(mine_rows, up_part, down_part)
    give, up_theirs, down_theirs = expert_math(their_rows, up_part, down_part)
    grad_up = up_mine + up_theirs
    grad_down = down_mine + down_theirs
    reduced = dp_reduce_scatter(keep, give, groups)
    reduced_low = reduced.astype(jnp.bfloat16)
    from_partner = partner(reduced_low[1], "expert", 0)
    total = reduced[0] + from_partner.astype(jnp.float32)
    map_f32 = lax.dynamic_index_in_dim(slot_map, parity, 0, keepdims=False)
    dx_total = total[:, :width].reshape(half_cap, 2, width // 2)
    spread = jnp.einsum("ij,isd->jsd", map_f32, dx_total, precision=highest)
    returned = lax.all_to_all(
        spread.astype(jnp.bfloat16), "expert", split_axis=0, concat_axis=0, tiled=True
    ).astype(jnp.float32)
    take_back = picked.reshape(owners, tok_local)
    in_grad = jnp.einsum("kl,ksd->lsd", take_back, returned, precision=highest)
    in_grad = in_grad.reshape(tok_local, width)
    gate_out = total[:, width].reshape(1, 1, half_cap)
    return (
        in_grad.astype(jnp.bfloat16),
        grad_up.astype(jnp.bfloat16)[None],
        grad_down.astype(jnp.bfloat16)[None],
        gate_out,
    )


def solution(mesh):
    placed = (
        P(("dp", "expert"), None),
        P(("dp", "expert"), None),
        P("dp", None, None),
        P("dp", None),
        P("dp", None, None),
        P("expert", None, "dp"),
        P("expert", "dp", None),
    )
    return jax.shard_map(
        on_device,
        mesh=mesh,
        in_specs=placed,
        out_specs=(
            P(("dp", "expert"), None),
            P("expert", None, "dp"),
            P("expert", "dp", None),
            P("dp", "expert", None),
        ),
        check_vma=False,
    )
```

```python
import jax
import jax.numpy as jnp
from jax import lax
from jax.sharding import PartitionSpec as P

root_two_over_pi = 0.7978845608028654
cubic_coef = 0.044715


def partner(x, axis, apart):
    return lax.ppermute(x, axis, [(i, i ^ 1 << apart) for i in range(lax.axis_size(axis))])


def dp_shift(x, step, groups):
    chips = groups // 2
    pairs = [(i, ((i // 2 + step) % chips) * 2 + i % 2) for i in range(groups)]
    return lax.ppermute(x, "dp", pairs)


def dp_all_gather(block, groups):
    chips = groups // 2
    chip = lax.axis_index("dp") // 2
    by_step = jnp.stack([block] + [dp_shift(block, step, groups) for step in range(1, chips)])
    mine = jnp.stack(
        [
            lax.dynamic_index_in_dim(by_step, (chip - place) % chips, 0, keepdims=False)
            for place in range(chips)
        ]
    )
    return mine, partner(mine, "dp", 0)


def dp_reduce_scatter(keep, give, groups):
    chips = groups // 2
    chip = lax.axis_index("dp") // 2
    got = partner(give, "dp", 0)
    pair_sum = keep.astype(jnp.float32) + got.astype(jnp.float32)
    pair_low = pair_sum.astype(jnp.bfloat16)
    total = lax.dynamic_index_in_dim(pair_sum, chip, 0, keepdims=False)
    for step in range(1, chips):
        piece = lax.dynamic_index_in_dim(pair_low, (chip + step) % chips, 0, keepdims=False)
        total = total + dp_shift(piece, step, groups).astype(jnp.float32)
    return total


def expert_math(chunk, up_part, down_part):
    width = up_part.shape[0]
    rows = chunk.reshape(-1, chunk.shape[-1])
    flat_x = rows[:, :width]
    flat_g = rows[:, width : 2 * width]
    flat_gate = rows[:, 2 * width].astype(jnp.float32)
    pre_act = jnp.dot(flat_x, up_part, preferred_element_type=jnp.float32)
    act_value, act_slope = gelu_pair(pre_act)
    hidden = act_value.astype(jnp.bfloat16)
    back_grad = lax.dot_general(
        flat_g, down_part, (((1,), (1,)), ((), ())), preferred_element_type=jnp.float32
    )
    gate_terms = jnp.sum(hidden.astype(jnp.float32) * back_grad, axis=1)
    scaled = (flat_gate[:, None] * flat_g.astype(jnp.float32)).astype(jnp.bfloat16)
    pre_grad = (flat_gate[:, None] * back_grad * act_slope).astype(jnp.bfloat16)
    dx_terms = lax.dot_general(
        pre_grad, up_part, (((1,), (1,)), ((), ())), preferred_element_type=jnp.float32
    )
    dx_low = dx_terms.astype(jnp.bfloat16)
    gate_low = jnp.pad(gate_terms.astype(jnp.bfloat16)[:, None], ((0, 0), (0, 127)))
    terms = jnp.concatenate([dx_low, gate_low], axis=1)
    terms = terms.reshape(chunk.shape[:-1] + (terms.shape[-1],))
    grad_down = lax.dot_general(
        hidden, scaled, (((0,), (0,)), ((), ())), preferred_element_type=jnp.float32
    )
    grad_up = lax.dot_general(
        flat_x, pre_grad, (((0,), (0,)), ((), ())), preferred_element_type=jnp.float32
    )
    return terms, grad_up, grad_down


def gelu_pair(pre_act):
    inner_arg = root_two_over_pi * (pre_act + cubic_coef * pre_act * pre_act * pre_act)
    tangent = jnp.tanh(inner_arg)
    act_value = 0.5 * pre_act * (1.0 + tangent)
    act_slope = 0.5 * (1.0 + tangent) + 0.5 * pre_act * (
        1.0 - tangent * tangent
    ) * root_two_over_pi * (1.0 + 3.0 * cubic_coef * pre_act * pre_act)
    return (act_value, act_slope)


def on_device(tokens_in, out_grad, chosen, counts, gates, w_up, w_down):
    tok_local = tokens_in.shape[0]
    width = tokens_in.shape[1]
    owners = lax.axis_size("expert")
    groups = lax.axis_size("dp")
    capacity = chosen.shape[2]
    half_cap = capacity // 2
    num_experts = chosen.shape[1]
    device = lax.axis_index("expert")
    expert = device // 2
    parity = device % 2
    my_lists = chosen[0]
    slot_ids = jnp.arange(capacity, dtype=jnp.int32)
    is_valid = slot_ids[None, :] < counts[0][:, None]
    owner_of = my_lists // tok_local
    local_of = my_lists % tok_local
    mine = jnp.logical_and(owner_of == device, is_valid)
    local_ids = jnp.arange(tok_local, dtype=jnp.int32)
    hits = jnp.logical_and(mine[:, :, None], local_of[:, :, None] == local_ids[None, None, :])
    hits_f = hits.astype(jnp.float32)
    picked = jnp.stack(
        [jnp.sum(hits_f[:, :half_cap], axis=1), jnp.sum(hits_f[:, half_cap:], axis=1)], axis=1
    )
    picked_low = picked.astype(jnp.bfloat16)
    list_row = lax.dynamic_index_in_dim(my_lists, expert, 0, keepdims=False)
    count_here = lax.dynamic_index_in_dim(counts[0], expert, 0, keepdims=False)
    valid_here = slot_ids < count_here
    gate_here = jnp.where(
        valid_here,
        lax.dynamic_index_in_dim(gates[0], expert, 0, keepdims=False),
        jnp.zeros((), jnp.bfloat16),
    )
    owner_ids = jnp.arange(owners, dtype=jnp.int32)
    slot_map = jnp.logical_and(
        (list_row // tok_local)[:, None] == owner_ids[None, :], valid_here[:, None]
    )
    slot_map = slot_map.astype(jnp.float32).reshape(2, half_cap, owners)
    map_low = slot_map.astype(jnp.bfloat16)
    gate_rows = gate_here.reshape(2, half_cap)
    both = jnp.stack([tokens_in, out_grad])
    send_xg = jnp.einsum(
        "erl,sld->ersd", picked_low, both, preferred_element_type=jnp.float32
    ).astype(jnp.bfloat16)
    send_xg = send_xg.reshape(owners, 2, width)
    recv_xg = lax.all_to_all(send_xg, "expert", split_axis=0, concat_axis=0, tiled=True)
    map_mine = lax.dynamic_index_in_dim(map_low, parity, 0, keepdims=False)
    rows_mine = jnp.einsum(
        "ij,jsd->isd", map_mine, recv_xg, preferred_element_type=jnp.float32
    ).astype(jnp.bfloat16)
    rows_mine = rows_mine.reshape(half_cap, 2 * width)
    rows_other = partner(rows_mine, "expert", 0)
    gate_mine = lax.dynamic_index_in_dim(gate_rows, parity, 0, keepdims=False)
    gate_other = lax.dynamic_index_in_dim(gate_rows, 1 - parity, 0, keepdims=False)
    rows_xg = jnp.stack([rows_mine, rows_other])
    gate_ord = jnp.stack([gate_mine, gate_other])
    gate_col = jnp.pad(gate_ord[:, :, None], ((0, 0), (0, 0), (0, 127)))
    packed = jnp.concatenate([rows_xg, gate_col], axis=2)
    mine_rows, their_rows = dp_all_gather(packed, groups)
    up_part = w_up[0]
    down_part = w_down[0]
    keep, up_mine, down_mine = expert_math(mine_rows, up_part, down_part)
    give, up_theirs, down_theirs = expert_math(their_rows, up_part, down_part)
    grad_up = up_mine + up_theirs
    grad_down = down_mine + down_theirs
    reduced = dp_reduce_scatter(keep, give, groups)
    reduced_low = reduced.astype(jnp.bfloat16)
    from_partner = partner(reduced_low[1], "expert", 0)
    total = reduced[0] + from_partner.astype(jnp.float32)
    dx_total = total[:, :width].astype(jnp.bfloat16).reshape(half_cap, 2, width // 2)
    spread = jnp.einsum(
        "ij,isd->jsd", map_mine, dx_total, preferred_element_type=jnp.float32
    ).astype(jnp.bfloat16)
    returned = lax.all_to_all(spread, "expert", split_axis=0, concat_axis=0, tiled=True)
    take_back = picked_low.reshape(owners, tok_local)
    in_grad = jnp.einsum(
        "kl,ksd->lsd", take_back, returned, preferred_element_type=jnp.float32
    )
    in_grad = in_grad.reshape(tok_local, width)
    gate_out = total[:, width].reshape(1, 1, half_cap)
    return (
        in_grad.astype(jnp.bfloat16),
        grad_up.astype(jnp.bfloat16)[None],
        grad_down.astype(jnp.bfloat16)[None],
        gate_out,
    )


def solution(mesh):
    placed = (
        P(("dp", "expert"), None),
        P(("dp", "expert"), None),
        P("dp", None, None),
        P("dp", None),
        P("dp", None, None),
        P("expert", None, "dp"),
        P("expert", "dp", None),
    )
    return jax.shard_map(
        on_device,
        mesh=mesh,
        in_specs=placed,
        out_specs=(
            P(("dp", "expert"), None),
            P("expert", None, "dp"),
            P("expert", "dp", None),
            P("dp", "expert", None),
        ),
        check_vma=False,
    )
```

```python
import jax
import jax.numpy as jnp
from jax import lax
from jax.sharding import PartitionSpec as P

root_two_over_pi = 0.7978845608028654
cubic_coef = 0.044715


def partner(x, axis, apart):
    return lax.ppermute(x, axis, [(i, i ^ 1 << apart) for i in range(lax.axis_size(axis))])


def dp_shift(x, step, groups):
    chips = groups // 2
    pairs = [(i, ((i // 2 + step) % chips) * 2 + i % 2) for i in range(groups)]
    return lax.ppermute(x, "dp", pairs)


def dp_all_gather(block, groups):
    chips = groups // 2
    chip = lax.axis_index("dp") // 2
    by_step = jnp.stack([block] + [dp_shift(block, step, groups) for step in range(1, chips)])
    mine = jnp.stack(
        [
            lax.dynamic_index_in_dim(by_step, (chip - place) % chips, 0, keepdims=False)
            for place in range(chips)
        ]
    )
    return mine, partner(mine, "dp", 0)


def dp_reduce_scatter(keep, give, groups):
    chips = groups // 2
    chip = lax.axis_index("dp") // 2
    got = partner(give, "dp", 0)
    pair_sum = keep.astype(jnp.float32) + got.astype(jnp.float32)
    pair_low = pair_sum.astype(jnp.bfloat16)
    total = lax.dynamic_index_in_dim(pair_sum, chip, 0, keepdims=False)
    for step in range(1, chips):
        piece = lax.dynamic_index_in_dim(pair_low, (chip + step) % chips, 0, keepdims=False)
        total = total + dp_shift(piece, step, groups).astype(jnp.float32)
    return total


def expert_math(chunk, up_part, down_part):
    width = up_part.shape[0]
    rows = chunk.reshape(-1, chunk.shape[-1])
    flat_x = rows[:, :width]
    flat_g = rows[:, width : 2 * width]
    flat_gate = rows[:, 2 * width].astype(jnp.float32)
    pre_act = jnp.dot(flat_x, up_part, preferred_element_type=jnp.float32)
    act_value, act_slope = gelu_pair(pre_act)
    hidden = act_value.astype(jnp.bfloat16)
    back_grad = lax.dot_general(
        flat_g, down_part, (((1,), (1,)), ((), ())), preferred_element_type=jnp.float32
    )
    gate_terms = jnp.sum(hidden.astype(jnp.float32) * back_grad, axis=1)
    scaled = (flat_gate[:, None] * flat_g.astype(jnp.float32)).astype(jnp.bfloat16)
    pre_grad = (flat_gate[:, None] * back_grad * act_slope).astype(jnp.bfloat16)
    dx_terms = lax.dot_general(
        pre_grad, up_part, (((1,), (1,)), ((), ())), preferred_element_type=jnp.float32
    )
    dx_low = dx_terms.astype(jnp.bfloat16)
    gate_low = jnp.pad(gate_terms.astype(jnp.bfloat16)[:, None], ((0, 0), (0, 127)))
    terms = jnp.concatenate([dx_low, gate_low], axis=1)
    terms = terms.reshape(chunk.shape[:-1] + (terms.shape[-1],))
    grad_down = lax.dot_general(
        hidden, scaled, (((0,), (0,)), ((), ())), preferred_element_type=jnp.float32
    )
    grad_up = lax.dot_general(
        flat_x, pre_grad, (((0,), (0,)), ((), ())), preferred_element_type=jnp.float32
    )
    return terms, grad_up, grad_down


def gelu_pair(pre_act):
    inner_arg = root_two_over_pi * (pre_act + cubic_coef * pre_act * pre_act * pre_act)
    tangent = jnp.tanh(inner_arg)
    act_value = 0.5 * pre_act * (1.0 + tangent)
    act_slope = 0.5 * (1.0 + tangent) + 0.5 * pre_act * (
        1.0 - tangent * tangent
    ) * root_two_over_pi * (1.0 + 3.0 * cubic_coef * pre_act * pre_act)
    return (act_value, act_slope)


def on_device(tokens_in, out_grad, chosen, counts, gates, w_up, w_down):
    tok_local = tokens_in.shape[0]
    width = tokens_in.shape[1]
    owners = lax.axis_size("expert")
    groups = lax.axis_size("dp")
    capacity = chosen.shape[2]
    half_cap = capacity // 2
    num_experts = chosen.shape[1]
    device = lax.axis_index("expert")
    expert = device // 2
    parity = device % 2
    my_lists = chosen[0]
    slot_ids = jnp.arange(capacity, dtype=jnp.int32)
    is_valid = slot_ids[None, :] < counts[0][:, None]
    owner_of = my_lists // tok_local
    local_of = my_lists % tok_local
    mine = jnp.logical_and(owner_of == device, is_valid)
    local_ids = jnp.arange(tok_local, dtype=jnp.int32)
    hits = jnp.logical_and(mine[:, :, None], local_of[:, :, None] == local_ids[None, None, :])
    hits_f = hits.astype(jnp.float32)
    picked = jnp.stack(
        [jnp.sum(hits_f[:, :half_cap], axis=1), jnp.sum(hits_f[:, half_cap:], axis=1)], axis=1
    )
    picked_low = picked.astype(jnp.bfloat16)
    list_row = lax.dynamic_index_in_dim(my_lists, expert, 0, keepdims=False)
    count_here = lax.dynamic_index_in_dim(counts[0], expert, 0, keepdims=False)
    valid_here = slot_ids < count_here
    gate_here = jnp.where(
        valid_here,
        lax.dynamic_index_in_dim(gates[0], expert, 0, keepdims=False),
        jnp.zeros((), jnp.bfloat16),
    )
    owner_ids = jnp.arange(owners, dtype=jnp.int32)
    slot_map = jnp.logical_and(
        (list_row // tok_local)[:, None] == owner_ids[None, :], valid_here[:, None]
    )
    slot_map = slot_map.astype(jnp.float32).reshape(2, half_cap, owners)
    map_low = slot_map.astype(jnp.bfloat16)
    gate_rows = gate_here.reshape(2, half_cap)
    both = jnp.stack([tokens_in, out_grad])
    send_xg = jnp.einsum(
        "erl,sld->ersd", picked_low, both, preferred_element_type=jnp.float32
    ).astype(jnp.bfloat16)
    send_xg = send_xg.reshape(owners, 2, width)
    recv_xg = lax.all_to_all(send_xg, "expert", split_axis=0, concat_axis=0, tiled=True)
    map_mine = lax.dynamic_index_in_dim(map_low, parity, 0, keepdims=False)
    rows_mine = jnp.einsum(
        "ij,jsd->isd", map_mine, recv_xg, preferred_element_type=jnp.float32
    ).astype(jnp.bfloat16)
    rows_mine = rows_mine.reshape(half_cap, 2 * width)
    rows_other = partner(rows_mine, "expert", 0)
    gate_mine = lax.dynamic_index_in_dim(gate_rows, parity, 0, keepdims=False)
    gate_other = lax.dynamic_index_in_dim(gate_rows, 1 - parity, 0, keepdims=False)
    rows_xg = jnp.stack([rows_mine, rows_other])
    gate_ord = jnp.stack([gate_mine, gate_other])
    gate_col = jnp.pad(gate_ord[:, :, None], ((0, 0), (0, 0), (0, 127)))
    packed = jnp.concatenate([rows_xg, gate_col], axis=2)
    mine_rows, their_rows = dp_all_gather(packed, groups)
    up_part = w_up[0]
    down_part = w_down[0]
    keep, up_mine, down_mine = expert_math(mine_rows, up_part, down_part)
    keep, up_mine, down_mine, their_rows = lax.optimization_barrier(
        (keep, up_mine, down_mine, their_rows)
    )
    give, up_theirs, down_theirs = expert_math(their_rows, up_part, down_part)
    grad_up = up_mine + up_theirs
    grad_down = down_mine + down_theirs
    reduced = dp_reduce_scatter(keep, give, groups)
    reduced_low = reduced.astype(jnp.bfloat16)
    from_partner = partner(reduced_low[1], "expert", 0)
    total = reduced[0] + from_partner.astype(jnp.float32)
    dx_total = total[:, :width].astype(jnp.bfloat16).reshape(half_cap, 2, width // 2)
    spread = jnp.einsum(
        "ij,isd->jsd", map_mine, dx_total, preferred_element_type=jnp.float32
    ).astype(jnp.bfloat16)
    returned = lax.all_to_all(spread, "expert", split_axis=0, concat_axis=0, tiled=True)
    take_back = picked_low.reshape(owners, tok_local)
    in_grad = jnp.einsum(
        "kl,ksd->lsd", take_back, returned, preferred_element_type=jnp.float32
    )
    in_grad = in_grad.reshape(tok_local, width)
    gate_out = total[:, width].reshape(1, 1, half_cap)
    return (
        in_grad.astype(jnp.bfloat16),
        grad_up.astype(jnp.bfloat16)[None],
        grad_down.astype(jnp.bfloat16)[None],
        gate_out,
    )


def solution(mesh):
    placed = (
        P(("dp", "expert"), None),
        P(("dp", "expert"), None),
        P("dp", None, None),
        P("dp", None),
        P("dp", None, None),
        P("expert", None, "dp"),
        P("expert", "dp", None),
    )
    return jax.shard_map(
        on_device,
        mesh=mesh,
        in_specs=placed,
        out_specs=(
            P(("dp", "expert"), None),
            P("expert", None, "dp"),
            P("expert", "dp", None),
            P("dp", "expert", None),
        ),
        check_vma=False,
    )
```

```python
import jax
import jax.numpy as jnp
from jax import lax
from jax.sharding import PartitionSpec as P

root_two_over_pi = 0.7978845608028654
cubic_coef = 0.044715


def partner(x, axis, apart):
    return lax.ppermute(x, axis, [(i, i ^ 1 << apart) for i in range(lax.axis_size(axis))])


def dp_shift(x, step, groups):
    chips = groups // 2
    pairs = [(i, ((i // 2 + step) % chips) * 2 + i % 2) for i in range(groups)]
    return lax.ppermute(x, "dp", pairs)


def same_core_groups(groups):
    return [list(range(core, groups, 2)) for core in range(2)]


def dp_all_gather(block, groups):
    chips = groups // 2
    copies = jnp.broadcast_to(block[None], (chips,) + block.shape)
    mine = lax.all_to_all(
        copies, "dp", 0, 0, axis_index_groups=same_core_groups(groups), tiled=True
    )
    return mine, partner(mine, "dp", 0)


def dp_reduce_scatter(keep, give, groups):
    got = partner(give, "dp", 0)
    pair_sum = keep.astype(jnp.float32) + got.astype(jnp.float32)
    pieces = lax.all_to_all(
        pair_sum.astype(jnp.bfloat16),
        "dp",
        0,
        0,
        axis_index_groups=same_core_groups(groups),
        tiled=True,
    )
    return jnp.sum(pieces.astype(jnp.float32), axis=0)


def expert_math(chunk, up_part, down_part):
    width = up_part.shape[0]
    rows = chunk.reshape(-1, chunk.shape[-1])
    flat_x = rows[:, :width]
    flat_g = rows[:, width : 2 * width]
    flat_gate = rows[:, 2 * width].astype(jnp.float32)
    pre_act = jnp.dot(flat_x, up_part, preferred_element_type=jnp.float32)
    act_value, act_slope = gelu_pair(pre_act)
    hidden = act_value.astype(jnp.bfloat16)
    back_grad = lax.dot_general(
        flat_g, down_part, (((1,), (1,)), ((), ())), preferred_element_type=jnp.float32
    )
    gate_terms = jnp.sum(hidden.astype(jnp.float32) * back_grad, axis=1)
    scaled = (flat_gate[:, None] * flat_g.astype(jnp.float32)).astype(jnp.bfloat16)
    pre_grad = (flat_gate[:, None] * back_grad * act_slope).astype(jnp.bfloat16)
    dx_terms = lax.dot_general(
        pre_grad, up_part, (((1,), (1,)), ((), ())), preferred_element_type=jnp.float32
    )
    dx_low = dx_terms.astype(jnp.bfloat16)
    gate_low = jnp.pad(gate_terms.astype(jnp.bfloat16)[:, None], ((0, 0), (0, 127)))
    terms = jnp.concatenate([dx_low, gate_low], axis=1)
    terms = terms.reshape(chunk.shape[:-1] + (terms.shape[-1],))
    grad_down = lax.dot_general(
        hidden, scaled, (((0,), (0,)), ((), ())), preferred_element_type=jnp.float32
    )
    grad_up = lax.dot_general(
        flat_x, pre_grad, (((0,), (0,)), ((), ())), preferred_element_type=jnp.float32
    )
    return terms, grad_up, grad_down


def gelu_pair(pre_act):
    inner_arg = root_two_over_pi * (pre_act + cubic_coef * pre_act * pre_act * pre_act)
    tangent = jnp.tanh(inner_arg)
    act_value = 0.5 * pre_act * (1.0 + tangent)
    act_slope = 0.5 * (1.0 + tangent) + 0.5 * pre_act * (
        1.0 - tangent * tangent
    ) * root_two_over_pi * (1.0 + 3.0 * cubic_coef * pre_act * pre_act)
    return (act_value, act_slope)


def on_device(tokens_in, out_grad, chosen, counts, gates, w_up, w_down):
    tok_local = tokens_in.shape[0]
    width = tokens_in.shape[1]
    owners = lax.axis_size("expert")
    groups = lax.axis_size("dp")
    capacity = chosen.shape[2]
    half_cap = capacity // 2
    num_experts = chosen.shape[1]
    device = lax.axis_index("expert")
    expert = device // 2
    parity = device % 2
    my_lists = chosen[0]
    slot_ids = jnp.arange(capacity, dtype=jnp.int32)
    is_valid = slot_ids[None, :] < counts[0][:, None]
    owner_of = my_lists // tok_local
    local_of = my_lists % tok_local
    mine = jnp.logical_and(owner_of == device, is_valid)
    local_ids = jnp.arange(tok_local, dtype=jnp.int32)
    hits = jnp.logical_and(mine[:, :, None], local_of[:, :, None] == local_ids[None, None, :])
    hits_f = hits.astype(jnp.float32)
    picked = jnp.stack(
        [jnp.sum(hits_f[:, :half_cap], axis=1), jnp.sum(hits_f[:, half_cap:], axis=1)], axis=1
    )
    picked_low = picked.astype(jnp.bfloat16)
    list_row = lax.dynamic_index_in_dim(my_lists, expert, 0, keepdims=False)
    count_here = lax.dynamic_index_in_dim(counts[0], expert, 0, keepdims=False)
    valid_here = slot_ids < count_here
    gate_here = jnp.where(
        valid_here,
        lax.dynamic_index_in_dim(gates[0], expert, 0, keepdims=False),
        jnp.zeros((), jnp.bfloat16),
    )
    owner_ids = jnp.arange(owners, dtype=jnp.int32)
    slot_map = jnp.logical_and(
        (list_row // tok_local)[:, None] == owner_ids[None, :], valid_here[:, None]
    )
    slot_map = slot_map.astype(jnp.float32).reshape(2, half_cap, owners)
    map_low = slot_map.astype(jnp.bfloat16)
    gate_rows = gate_here.reshape(2, half_cap)
    both = jnp.stack([tokens_in, out_grad])
    send_xg = jnp.einsum(
        "erl,sld->ersd", picked_low, both, preferred_element_type=jnp.float32
    ).astype(jnp.bfloat16)
    send_xg = send_xg.reshape(owners, 2, width)
    recv_xg = lax.all_to_all(send_xg, "expert", split_axis=0, concat_axis=0, tiled=True)
    map_mine = lax.dynamic_index_in_dim(map_low, parity, 0, keepdims=False)
    rows_mine = jnp.einsum(
        "ij,jsd->isd", map_mine, recv_xg, preferred_element_type=jnp.float32
    ).astype(jnp.bfloat16)
    rows_mine = rows_mine.reshape(half_cap, 2 * width)
    rows_other = partner(rows_mine, "expert", 0)
    gate_mine = lax.dynamic_index_in_dim(gate_rows, parity, 0, keepdims=False)
    gate_other = lax.dynamic_index_in_dim(gate_rows, 1 - parity, 0, keepdims=False)
    rows_xg = jnp.stack([rows_mine, rows_other])
    gate_ord = jnp.stack([gate_mine, gate_other])
    gate_col = jnp.pad(gate_ord[:, :, None], ((0, 0), (0, 0), (0, 127)))
    packed = jnp.concatenate([rows_xg, gate_col], axis=2)
    mine_rows, their_rows = dp_all_gather(packed, groups)
    up_part = w_up[0]
    down_part = w_down[0]
    keep, up_mine, down_mine = expert_math(mine_rows, up_part, down_part)
    give, up_theirs, down_theirs = expert_math(their_rows, up_part, down_part)
    grad_up = up_mine + up_theirs
    grad_down = down_mine + down_theirs
    reduced = dp_reduce_scatter(keep, give, groups)
    reduced_low = reduced.astype(jnp.bfloat16)
    from_partner = partner(reduced_low[1], "expert", 0)
    total = reduced[0] + from_partner.astype(jnp.float32)
    dx_total = total[:, :width].astype(jnp.bfloat16).reshape(half_cap, 2, width // 2)
    spread = jnp.einsum(
        "ij,isd->jsd", map_mine, dx_total, preferred_element_type=jnp.float32
    ).astype(jnp.bfloat16)
    returned = lax.all_to_all(spread, "expert", split_axis=0, concat_axis=0, tiled=True)
    take_back = picked_low.reshape(owners, tok_local)
    in_grad = jnp.einsum(
        "kl,ksd->lsd", take_back, returned, preferred_element_type=jnp.float32
    )
    in_grad = in_grad.reshape(tok_local, width)
    gate_out = total[:, width].reshape(1, 1, half_cap)
    return (
        in_grad.astype(jnp.bfloat16),
        grad_up.astype(jnp.bfloat16)[None],
        grad_down.astype(jnp.bfloat16)[None],
        gate_out,
    )


def solution(mesh):
    placed = (
        P(("dp", "expert"), None),
        P(("dp", "expert"), None),
        P("dp", None, None),
        P("dp", None),
        P("dp", None, None),
        P("expert", None, "dp"),
        P("expert", "dp", None),
    )
    return jax.shard_map(
        on_device,
        mesh=mesh,
        in_specs=placed,
        out_specs=(
            P(("dp", "expert"), None),
            P("expert", None, "dp"),
            P("expert", "dp", None),
            P("dp", "expert", None),
        ),
        check_vma=False,
    )
```

```python
import jax
import jax.numpy as jnp
from jax import lax
from jax.sharding import PartitionSpec as P

root_two_over_pi = 0.7978845608028654
cubic_coef = 0.044715


def partner(x, axis, apart):
    return lax.ppermute(x, axis, [(i, i ^ 1 << apart) for i in range(lax.axis_size(axis))])


def dp_shift(x, step, groups):
    chips = groups // 2
    pairs = [(i, ((i // 2 + step) % chips) * 2 + i % 2) for i in range(groups)]
    return lax.ppermute(x, "dp", pairs)


def same_core_groups(groups):
    return [list(range(core, groups, 2)) for core in range(2)]


def block_groups(groups, owners):
    return [
        [(2 * chip + core) * owners + 2 * pair + half for chip in range(groups // 2) for half in range(2)]
        for core in range(2)
        for pair in range(owners // 2)
    ]


def dp_all_gather(block, groups, owners):
    copies = jnp.broadcast_to(block[None], (groups,) + block.shape)
    mine = lax.all_to_all(
        copies, ("dp", "expert"), 0, 0, axis_index_groups=block_groups(groups, owners), tiled=True
    )
    mine = mine.reshape((groups // 2, 2) + block.shape)
    return mine, partner(mine, "dp", 0)


def dp_reduce_scatter(keep, give, groups, owners):
    got = partner(give, "dp", 0)
    pair_sum = keep.astype(jnp.float32) + got.astype(jnp.float32)
    pair_sum = pair_sum.reshape((groups,) + pair_sum.shape[2:])
    pieces = lax.all_to_all(
        pair_sum.astype(jnp.bfloat16),
        ("dp", "expert"),
        0,
        0,
        axis_index_groups=block_groups(groups, owners),
        tiled=True,
    )
    return jnp.sum(pieces.astype(jnp.float32), axis=0)


def expert_math(chunk, up_part, down_part):
    width = up_part.shape[0]
    rows = chunk.reshape(-1, chunk.shape[-1])
    flat_x = rows[:, :width]
    flat_g = rows[:, width : 2 * width]
    flat_gate = rows[:, 2 * width].astype(jnp.float32)
    pre_act = jnp.dot(flat_x, up_part, preferred_element_type=jnp.float32)
    act_value, act_slope = gelu_pair(pre_act)
    hidden = act_value.astype(jnp.bfloat16)
    back_grad = lax.dot_general(
        flat_g, down_part, (((1,), (1,)), ((), ())), preferred_element_type=jnp.float32
    )
    gate_terms = jnp.sum(hidden.astype(jnp.float32) * back_grad, axis=1)
    scaled = (flat_gate[:, None] * flat_g.astype(jnp.float32)).astype(jnp.bfloat16)
    pre_grad = (flat_gate[:, None] * back_grad * act_slope).astype(jnp.bfloat16)
    dx_terms = lax.dot_general(
        pre_grad, up_part, (((1,), (1,)), ((), ())), preferred_element_type=jnp.float32
    )
    dx_low = dx_terms.astype(jnp.bfloat16)
    gate_low = jnp.pad(gate_terms.astype(jnp.bfloat16)[:, None], ((0, 0), (0, 127)))
    terms = jnp.concatenate([dx_low, gate_low], axis=1)
    terms = terms.reshape(chunk.shape[:-1] + (terms.shape[-1],))
    grad_down = lax.dot_general(
        hidden, scaled, (((0,), (0,)), ((), ())), preferred_element_type=jnp.float32
    )
    grad_up = lax.dot_general(
        flat_x, pre_grad, (((0,), (0,)), ((), ())), preferred_element_type=jnp.float32
    )
    return terms, grad_up, grad_down


def gelu_pair(pre_act):
    inner_arg = root_two_over_pi * (pre_act + cubic_coef * pre_act * pre_act * pre_act)
    tangent = jnp.tanh(inner_arg)
    act_value = 0.5 * pre_act * (1.0 + tangent)
    act_slope = 0.5 * (1.0 + tangent) + 0.5 * pre_act * (
        1.0 - tangent * tangent
    ) * root_two_over_pi * (1.0 + 3.0 * cubic_coef * pre_act * pre_act)
    return (act_value, act_slope)


def on_device(tokens_in, out_grad, chosen, counts, gates, w_up, w_down):
    tok_local = tokens_in.shape[0]
    width = tokens_in.shape[1]
    owners = lax.axis_size("expert")
    groups = lax.axis_size("dp")
    capacity = chosen.shape[2]
    half_cap = capacity // 2
    num_experts = chosen.shape[1]
    device = lax.axis_index("expert")
    expert = device // 2
    parity = device % 2
    my_lists = chosen[0]
    slot_ids = jnp.arange(capacity, dtype=jnp.int32)
    is_valid = slot_ids[None, :] < counts[0][:, None]
    owner_of = my_lists // tok_local
    local_of = my_lists % tok_local
    mine = jnp.logical_and(owner_of == device, is_valid)
    local_ids = jnp.arange(tok_local, dtype=jnp.int32)
    hits = jnp.logical_and(mine[:, :, None], local_of[:, :, None] == local_ids[None, None, :])
    hits_f = hits.astype(jnp.float32)
    picked = jnp.stack(
        [jnp.sum(hits_f[:, :half_cap], axis=1), jnp.sum(hits_f[:, half_cap:], axis=1)], axis=1
    )
    picked_low = picked.astype(jnp.bfloat16)
    list_row = lax.dynamic_index_in_dim(my_lists, expert, 0, keepdims=False)
    count_here = lax.dynamic_index_in_dim(counts[0], expert, 0, keepdims=False)
    valid_here = slot_ids < count_here
    gate_here = jnp.where(
        valid_here,
        lax.dynamic_index_in_dim(gates[0], expert, 0, keepdims=False),
        jnp.zeros((), jnp.bfloat16),
    )
    owner_ids = jnp.arange(owners, dtype=jnp.int32)
    slot_map = jnp.logical_and(
        (list_row // tok_local)[:, None] == owner_ids[None, :], valid_here[:, None]
    )
    slot_map = slot_map.astype(jnp.float32).reshape(2, half_cap, owners)
    map_low = slot_map.astype(jnp.bfloat16)
    gate_rows = gate_here.reshape(2, half_cap)
    both = jnp.stack([tokens_in, out_grad])
    send_xg = jnp.einsum(
        "erl,sld->ersd", picked_low, both, preferred_element_type=jnp.float32
    ).astype(jnp.bfloat16)
    send_xg = send_xg.reshape(owners, 2, width)
    recv_xg = lax.all_to_all(send_xg, "expert", split_axis=0, concat_axis=0, tiled=True)
    map_mine = lax.dynamic_index_in_dim(map_low, parity, 0, keepdims=False)
    rows_mine = jnp.einsum(
        "ij,jsd->isd", map_mine, recv_xg, preferred_element_type=jnp.float32
    ).astype(jnp.bfloat16)
    rows_mine = rows_mine.reshape(half_cap, 2 * width)
    gate_mine = lax.dynamic_index_in_dim(gate_rows, parity, 0, keepdims=False)
    gate_col = jnp.pad(gate_mine[:, None], ((0, 0), (0, 127)))
    packed = jnp.concatenate([rows_mine, gate_col], axis=1)
    mine_rows, their_rows = dp_all_gather(packed, groups, owners)
    up_part = w_up[0]
    down_part = w_down[0]
    keep, up_mine, down_mine = expert_math(mine_rows, up_part, down_part)
    give, up_theirs, down_theirs = expert_math(their_rows, up_part, down_part)
    grad_up = up_mine + up_theirs
    grad_down = down_mine + down_theirs
    total = dp_reduce_scatter(keep, give, groups, owners)
    dx_total = total[:, :width].astype(jnp.bfloat16).reshape(half_cap, 2, width // 2)
    spread = jnp.einsum(
        "ij,isd->jsd", map_mine, dx_total, preferred_element_type=jnp.float32
    ).astype(jnp.bfloat16)
    returned = lax.all_to_all(spread, "expert", split_axis=0, concat_axis=0, tiled=True)
    take_back = picked_low.reshape(owners, tok_local)
    in_grad = jnp.einsum(
        "kl,ksd->lsd", take_back, returned, preferred_element_type=jnp.float32
    )
    in_grad = in_grad.reshape(tok_local, width)
    gate_out = total[:, width].reshape(1, 1, half_cap)
    return (
        in_grad.astype(jnp.bfloat16),
        grad_up.astype(jnp.bfloat16)[None],
        grad_down.astype(jnp.bfloat16)[None],
        gate_out,
    )


def solution(mesh):
    placed = (
        P(("dp", "expert"), None),
        P(("dp", "expert"), None),
        P("dp", None, None),
        P("dp", None),
        P("dp", None, None),
        P("expert", None, "dp"),
        P("expert", "dp", None),
    )
    return jax.shard_map(
        on_device,
        mesh=mesh,
        in_specs=placed,
        out_specs=(
            P(("dp", "expert"), None),
            P("expert", None, "dp"),
            P("expert", "dp", None),
            P("dp", "expert", None),
        ),
        check_vma=False,
    )
```

```python
import jax
import jax.numpy as jnp
from jax import lax
from jax.sharding import PartitionSpec as P

root_two_over_pi = 0.7978845608028654
cubic_coef = 0.044715


def partner(x, axis, apart):
    return lax.ppermute(x, axis, [(i, i ^ 1 << apart) for i in range(lax.axis_size(axis))])


def dp_shift(x, step, groups):
    chips = groups // 2
    pairs = [(i, ((i // 2 + step) % chips) * 2 + i % 2) for i in range(groups)]
    return lax.ppermute(x, "dp", pairs)


def same_core_groups(groups):
    return [list(range(core, groups, 2)) for core in range(2)]


def block_groups(groups, owners):
    return [
        [(2 * chip + core) * owners + 2 * pair + half for chip in range(groups // 2) for half in range(2)]
        for core in range(2)
        for pair in range(owners // 2)
    ]


def dp_all_gather(block, groups, owners):
    copies = jnp.broadcast_to(block[None], (groups,) + block.shape)
    mine = lax.all_to_all(
        copies, ("dp", "expert"), 0, 0, axis_index_groups=block_groups(groups, owners), tiled=True
    )
    mine = mine.reshape((groups // 2, 2) + block.shape)
    return mine, partner(mine, "dp", 0)


def dp_reduce_scatter(keep, got, groups, owners):
    pair_sum = keep.astype(jnp.float32) + got.astype(jnp.float32)
    pair_sum = pair_sum.reshape((groups,) + pair_sum.shape[2:])
    pieces = lax.all_to_all(
        pair_sum.astype(jnp.bfloat16),
        ("dp", "expert"),
        0,
        0,
        axis_index_groups=block_groups(groups, owners),
        tiled=True,
    )
    return jnp.sum(pieces.astype(jnp.float32), axis=0)


def expert_math(chunk, up_part, down_part):
    width = up_part.shape[0]
    rows = chunk.reshape(-1, chunk.shape[-1])
    flat_x = rows[:, :width]
    flat_g = rows[:, width : 2 * width]
    flat_gate = rows[:, 2 * width].astype(jnp.float32)
    pre_act = jnp.dot(flat_x, up_part, preferred_element_type=jnp.float32)
    act_value, act_slope = gelu_pair(pre_act)
    hidden = act_value.astype(jnp.bfloat16)
    back_grad = lax.dot_general(
        flat_g, down_part, (((1,), (1,)), ((), ())), preferred_element_type=jnp.float32
    )
    gate_terms = jnp.sum(hidden.astype(jnp.float32) * back_grad, axis=1)
    scaled = (flat_gate[:, None] * flat_g.astype(jnp.float32)).astype(jnp.bfloat16)
    pre_grad = (flat_gate[:, None] * back_grad * act_slope).astype(jnp.bfloat16)
    dx_terms = lax.dot_general(
        pre_grad, up_part, (((1,), (1,)), ((), ())), preferred_element_type=jnp.float32
    )
    dx_low = dx_terms.astype(jnp.bfloat16)
    gate_low = jnp.pad(gate_terms.astype(jnp.bfloat16)[:, None], ((0, 0), (0, 127)))
    terms = jnp.concatenate([dx_low, gate_low], axis=1)
    terms = terms.reshape(chunk.shape[:-1] + (terms.shape[-1],))
    grad_down = lax.dot_general(
        hidden, scaled, (((0,), (0,)), ((), ())), preferred_element_type=jnp.float32
    )
    grad_up = lax.dot_general(
        flat_x, pre_grad, (((0,), (0,)), ((), ())), preferred_element_type=jnp.float32
    )
    return terms, grad_up, grad_down


def gelu_pair(pre_act):
    inner_arg = root_two_over_pi * (pre_act + cubic_coef * pre_act * pre_act * pre_act)
    tangent = jnp.tanh(inner_arg)
    act_value = 0.5 * pre_act * (1.0 + tangent)
    act_slope = 0.5 * (1.0 + tangent) + 0.5 * pre_act * (
        1.0 - tangent * tangent
    ) * root_two_over_pi * (1.0 + 3.0 * cubic_coef * pre_act * pre_act)
    return (act_value, act_slope)


def on_device(tokens_in, out_grad, chosen, counts, gates, w_up, w_down):
    tok_local = tokens_in.shape[0]
    width = tokens_in.shape[1]
    owners = lax.axis_size("expert")
    groups = lax.axis_size("dp")
    capacity = chosen.shape[2]
    half_cap = capacity // 2
    num_experts = chosen.shape[1]
    device = lax.axis_index("expert")
    expert = device // 2
    parity = device % 2
    my_lists = chosen[0]
    slot_ids = jnp.arange(capacity, dtype=jnp.int32)
    is_valid = slot_ids[None, :] < counts[0][:, None]
    owner_of = my_lists // tok_local
    local_of = my_lists % tok_local
    mine = jnp.logical_and(owner_of == device, is_valid)
    local_ids = jnp.arange(tok_local, dtype=jnp.int32)
    hits = jnp.logical_and(mine[:, :, None], local_of[:, :, None] == local_ids[None, None, :])
    hits_f = hits.astype(jnp.float32)
    picked = jnp.stack(
        [jnp.sum(hits_f[:, :half_cap], axis=1), jnp.sum(hits_f[:, half_cap:], axis=1)], axis=1
    )
    picked_low = picked.astype(jnp.bfloat16)
    list_row = lax.dynamic_index_in_dim(my_lists, expert, 0, keepdims=False)
    count_here = lax.dynamic_index_in_dim(counts[0], expert, 0, keepdims=False)
    valid_here = slot_ids < count_here
    gate_here = jnp.where(
        valid_here,
        lax.dynamic_index_in_dim(gates[0], expert, 0, keepdims=False),
        jnp.zeros((), jnp.bfloat16),
    )
    owner_ids = jnp.arange(owners, dtype=jnp.int32)
    slot_map = jnp.logical_and(
        (list_row // tok_local)[:, None] == owner_ids[None, :], valid_here[:, None]
    )
    slot_map = slot_map.astype(jnp.float32).reshape(2, half_cap, owners)
    map_low = slot_map.astype(jnp.bfloat16)
    gate_rows = gate_here.reshape(2, half_cap)
    both = jnp.stack([tokens_in, out_grad])
    send_xg = jnp.einsum(
        "erl,sld->ersd", picked_low, both, preferred_element_type=jnp.float32
    ).astype(jnp.bfloat16)
    send_xg = send_xg.reshape(owners, 2, width)
    recv_xg = lax.all_to_all(send_xg, "expert", split_axis=0, concat_axis=0, tiled=True)
    map_mine = lax.dynamic_index_in_dim(map_low, parity, 0, keepdims=False)
    rows_mine = jnp.einsum(
        "ij,jsd->isd", map_mine, recv_xg, preferred_element_type=jnp.float32
    ).astype(jnp.bfloat16)
    rows_mine = rows_mine.reshape(half_cap, 2 * width)
    gate_mine = lax.dynamic_index_in_dim(gate_rows, parity, 0, keepdims=False)
    gate_col = jnp.pad(gate_mine[:, None], ((0, 0), (0, 127)))
    packed = jnp.concatenate([rows_mine, gate_col], axis=1)
    mine_rows, their_rows = dp_all_gather(packed, groups, owners)
    up_part = w_up[0]
    down_part = w_down[0]
    keep, up_mine, down_mine = expert_math(mine_rows, up_part, down_part)
    keep, their_rows = lax.optimization_barrier((keep, their_rows))
    give, up_theirs, down_theirs = expert_math(their_rows, up_part, down_part)
    got = partner(give, "dp", 0)
    got, up_mine, down_mine = lax.optimization_barrier((got, up_mine, down_mine))
    grad_up = up_mine + up_theirs
    grad_down = down_mine + down_theirs
    total = dp_reduce_scatter(keep, got, groups, owners)
    dx_total = total[:, :width].astype(jnp.bfloat16).reshape(half_cap, 2, width // 2)
    spread = jnp.einsum(
        "ij,isd->jsd", map_mine, dx_total, preferred_element_type=jnp.float32
    ).astype(jnp.bfloat16)
    returned = lax.all_to_all(spread, "expert", split_axis=0, concat_axis=0, tiled=True)
    take_back = picked_low.reshape(owners, tok_local)
    in_grad = jnp.einsum(
        "kl,ksd->lsd", take_back, returned, preferred_element_type=jnp.float32
    )
    in_grad = in_grad.reshape(tok_local, width)
    gate_out = total[:, width].reshape(1, 1, half_cap)
    return (
        in_grad.astype(jnp.bfloat16),
        grad_up.astype(jnp.bfloat16)[None],
        grad_down.astype(jnp.bfloat16)[None],
        gate_out,
    )


def solution(mesh):
    placed = (
        P(("dp", "expert"), None),
        P(("dp", "expert"), None),
        P("dp", None, None),
        P("dp", None),
        P("dp", None, None),
        P("expert", None, "dp"),
        P("expert", "dp", None),
    )
    return jax.shard_map(
        on_device,
        mesh=mesh,
        in_specs=placed,
        out_specs=(
            P(("dp", "expert"), None),
            P("expert", None, "dp"),
            P("expert", "dp", None),
            P("dp", "expert", None),
        ),
        check_vma=False,
    )
```

```python
import jax
import jax.numpy as jnp
from jax import lax
from jax.sharding import PartitionSpec as P

root_two_over_pi = 0.7978845608028654
cubic_coef = 0.044715


def partner(x, axis, apart):
    return lax.ppermute(x, axis, [(i, i ^ 1 << apart) for i in range(lax.axis_size(axis))])


def dp_shift(x, step, groups):
    chips = groups // 2
    pairs = [(i, ((i // 2 + step) % chips) * 2 + i % 2) for i in range(groups)]
    return lax.ppermute(x, "dp", pairs)


def same_core_groups(groups):
    return [list(range(core, groups, 2)) for core in range(2)]


def block_groups(groups, owners):
    return [
        [(2 * chip + core) * owners + 2 * pair + half for chip in range(groups // 2) for half in range(2)]
        for core in range(2)
        for pair in range(owners // 2)
    ]


def dp_all_gather(block, groups, owners):
    copies = jnp.broadcast_to(block[None], (groups,) + block.shape)
    mine = lax.all_to_all(
        copies, ("dp", "expert"), 0, 0, axis_index_groups=block_groups(groups, owners), tiled=True
    )
    mine = mine.reshape((groups // 2, 2) + block.shape)
    return mine, partner(mine, "dp", 0)


def dp_reduce_scatter(keep, got, groups, owners):
    pair_sum = keep.astype(jnp.float32) + got.astype(jnp.float32)
    pair_sum = pair_sum.reshape((groups,) + pair_sum.shape[2:])
    pieces = lax.all_to_all(
        pair_sum.astype(jnp.bfloat16),
        ("dp", "expert"),
        0,
        0,
        axis_index_groups=block_groups(groups, owners),
        tiled=True,
    )
    return pieces


def expert_math(chunk, up_part, down_part):
    width = up_part.shape[0]
    rows = chunk.reshape(-1, chunk.shape[-1])
    flat_x = rows[:, :width]
    flat_g = rows[:, width : 2 * width]
    flat_gate = rows[:, 2 * width].astype(jnp.float32)
    pre_act = jnp.dot(flat_x, up_part, preferred_element_type=jnp.float32)
    act_value, act_slope = gelu_pair(pre_act)
    hidden = act_value.astype(jnp.bfloat16)
    back_grad = lax.dot_general(
        flat_g, down_part, (((1,), (1,)), ((), ())), preferred_element_type=jnp.float32
    )
    gate_terms = jnp.sum(hidden.astype(jnp.float32) * back_grad, axis=1)
    scaled = (flat_gate[:, None] * flat_g.astype(jnp.float32)).astype(jnp.bfloat16)
    pre_grad = (flat_gate[:, None] * back_grad * act_slope).astype(jnp.bfloat16)
    dx_terms = lax.dot_general(
        pre_grad, up_part, (((1,), (1,)), ((), ())), preferred_element_type=jnp.float32
    )
    dx_low = dx_terms.astype(jnp.bfloat16)
    gate_low = jnp.pad(gate_terms.astype(jnp.bfloat16)[:, None], ((0, 0), (0, 127)))
    terms = jnp.concatenate([dx_low, gate_low], axis=1)
    terms = terms.reshape(chunk.shape[:-1] + (terms.shape[-1],))
    grad_down = lax.dot_general(
        hidden, scaled, (((0,), (0,)), ((), ())), preferred_element_type=jnp.float32
    )
    grad_up = lax.dot_general(
        flat_x, pre_grad, (((0,), (0,)), ((), ())), preferred_element_type=jnp.float32
    )
    return terms, grad_up, grad_down


def gelu_pair(pre_act):
    inner_arg = root_two_over_pi * (pre_act + cubic_coef * pre_act * pre_act * pre_act)
    tangent = jnp.tanh(inner_arg)
    act_value = 0.5 * pre_act * (1.0 + tangent)
    act_slope = 0.5 * (1.0 + tangent) + 0.5 * pre_act * (
        1.0 - tangent * tangent
    ) * root_two_over_pi * (1.0 + 3.0 * cubic_coef * pre_act * pre_act)
    return (act_value, act_slope)


def on_device(tokens_in, out_grad, chosen, counts, gates, w_up, w_down):
    tok_local = tokens_in.shape[0]
    width = tokens_in.shape[1]
    owners = lax.axis_size("expert")
    groups = lax.axis_size("dp")
    capacity = chosen.shape[2]
    half_cap = capacity // 2
    num_experts = chosen.shape[1]
    device = lax.axis_index("expert")
    expert = device // 2
    parity = device % 2
    my_lists = chosen[0]
    slot_ids = jnp.arange(capacity, dtype=jnp.int32)
    is_valid = slot_ids[None, :] < counts[0][:, None]
    owner_of = my_lists // tok_local
    local_of = my_lists % tok_local
    mine = jnp.logical_and(owner_of == device, is_valid)
    local_ids = jnp.arange(tok_local, dtype=jnp.int32)
    hits = jnp.logical_and(mine[:, :, None], local_of[:, :, None] == local_ids[None, None, :])
    hits_f = hits.astype(jnp.float32)
    picked = jnp.stack(
        [jnp.sum(hits_f[:, :half_cap], axis=1), jnp.sum(hits_f[:, half_cap:], axis=1)], axis=1
    )
    picked_low = picked.astype(jnp.bfloat16)
    list_row = lax.dynamic_index_in_dim(my_lists, expert, 0, keepdims=False)
    count_here = lax.dynamic_index_in_dim(counts[0], expert, 0, keepdims=False)
    valid_here = slot_ids < count_here
    gate_here = jnp.where(
        valid_here,
        lax.dynamic_index_in_dim(gates[0], expert, 0, keepdims=False),
        jnp.zeros((), jnp.bfloat16),
    )
    owner_ids = jnp.arange(owners, dtype=jnp.int32)
    slot_map = jnp.logical_and(
        (list_row // tok_local)[:, None] == owner_ids[None, :], valid_here[:, None]
    )
    slot_map = slot_map.astype(jnp.float32).reshape(2, half_cap, owners)
    map_low = slot_map.astype(jnp.bfloat16)
    gate_rows = gate_here.reshape(2, half_cap)
    both = jnp.stack([tokens_in, out_grad])
    send_xg = jnp.einsum(
        "erl,sld->ersd", picked_low, both, preferred_element_type=jnp.float32
    ).astype(jnp.bfloat16)
    send_xg = send_xg.reshape(owners, 2, width)
    recv_xg = lax.all_to_all(send_xg, "expert", split_axis=0, concat_axis=0, tiled=True)
    map_mine = lax.dynamic_index_in_dim(map_low, parity, 0, keepdims=False)
    rows_mine = jnp.einsum(
        "ij,jsd->isd", map_mine, recv_xg, preferred_element_type=jnp.float32
    ).astype(jnp.bfloat16)
    rows_mine = rows_mine.reshape(half_cap, 2 * width)
    gate_mine = lax.dynamic_index_in_dim(gate_rows, parity, 0, keepdims=False)
    gate_col = jnp.pad(gate_mine[:, None], ((0, 0), (0, 127)))
    packed = jnp.concatenate([rows_mine, gate_col], axis=1)
    mine_rows, their_rows = dp_all_gather(packed, groups, owners)
    up_part = w_up[0]
    down_part = w_down[0]
    keep, up_mine, down_mine = expert_math(mine_rows, up_part, down_part)
    keep, their_rows = lax.optimization_barrier((keep, their_rows))
    give, up_theirs, down_theirs = expert_math(their_rows, up_part, down_part)
    got = partner(give, "dp", 0)
    got, up_mine, down_mine = lax.optimization_barrier((got, up_mine, down_mine))
    grad_up = up_mine + up_theirs
    grad_down = down_mine + down_theirs
    pieces = dp_reduce_scatter(keep, got, groups, owners)
    dx_pieces = pieces[:, :, :width].reshape(groups, half_cap, 2, width // 2)
    spread = jnp.einsum(
        "ij,kisd->jsd", map_mine, dx_pieces, preferred_element_type=jnp.float32
    ).astype(jnp.bfloat16)
    returned = lax.all_to_all(spread, "expert", split_axis=0, concat_axis=0, tiled=True)
    take_back = picked_low.reshape(owners, tok_local)
    in_grad = jnp.einsum(
        "kl,ksd->lsd", take_back, returned, preferred_element_type=jnp.float32
    )
    in_grad = in_grad.reshape(tok_local, width)
    gate_out = jnp.sum(pieces[:, :, width].astype(jnp.float32), axis=0).reshape(1, 1, half_cap)
    return (
        in_grad.astype(jnp.bfloat16),
        grad_up.astype(jnp.bfloat16)[None],
        grad_down.astype(jnp.bfloat16)[None],
        gate_out,
    )


def solution(mesh):
    placed = (
        P(("dp", "expert"), None),
        P(("dp", "expert"), None),
        P("dp", None, None),
        P("dp", None),
        P("dp", None, None),
        P("expert", None, "dp"),
        P("expert", "dp", None),
    )
    return jax.shard_map(
        on_device,
        mesh=mesh,
        in_specs=placed,
        out_specs=(
            P(("dp", "expert"), None),
            P("expert", None, "dp"),
            P("expert", "dp", None),
            P("dp", "expert", None),
        ),
        check_vma=False,
    )
```

```python
import jax
import jax.numpy as jnp
from jax import lax
from jax.sharding import PartitionSpec as P

root_two_over_pi = 0.7978845608028654
cubic_coef = 0.044715


def partner(x, axis, apart):
    return lax.ppermute(x, axis, [(i, i ^ 1 << apart) for i in range(lax.axis_size(axis))])


def dp_shift(x, step, groups):
    chips = groups // 2
    pairs = [(i, ((i // 2 + step) % chips) * 2 + i % 2) for i in range(groups)]
    return lax.ppermute(x, "dp", pairs)


def same_core_groups(groups):
    return [list(range(core, groups, 2)) for core in range(2)]


def block_groups(groups, owners):
    return [
        [(2 * chip + core) * owners + 2 * pair + half for chip in range(groups // 2) for half in range(2)]
        for core in range(2)
        for pair in range(owners // 2)
    ]


def dp_all_gather(block, groups, owners):
    copies = jnp.broadcast_to(block[None], (groups,) + block.shape)
    mine = lax.all_to_all(
        copies, ("dp", "expert"), 0, 0, axis_index_groups=block_groups(groups, owners), tiled=True
    )
    mine = mine.reshape((groups // 2, 2) + block.shape)
    return mine, partner(mine, "dp", 0)


def dp_reduce_scatter(keep, got, groups, owners):
    pair_sum = keep.astype(jnp.float32) + got.astype(jnp.float32)
    pair_sum = pair_sum.reshape((groups,) + pair_sum.shape[2:])
    pieces = lax.all_to_all(
        pair_sum.astype(jnp.bfloat16),
        ("dp", "expert"),
        0,
        0,
        axis_index_groups=block_groups(groups, owners),
        tiled=True,
    )
    return pieces


def expert_math(chunk, up_part, down_part):
    width = up_part.shape[0]
    rows = chunk.reshape(-1, chunk.shape[-1])
    flat_x = rows[:, :width]
    flat_g = rows[:, width : 2 * width]
    flat_gate = rows[:, 2 * width].astype(jnp.float32)
    pre_act = jnp.dot(flat_x, up_part, preferred_element_type=jnp.float32)
    act_value, act_slope = gelu_pair(pre_act)
    hidden = act_value.astype(jnp.bfloat16)
    back_grad = lax.dot_general(
        flat_g, down_part, (((1,), (1,)), ((), ())), preferred_element_type=jnp.float32
    )
    gate_terms = jnp.sum(hidden.astype(jnp.float32) * back_grad, axis=1)
    scaled = (flat_gate[:, None] * flat_g.astype(jnp.float32)).astype(jnp.bfloat16)
    pre_grad = (flat_gate[:, None] * back_grad * act_slope).astype(jnp.bfloat16)
    dx_terms = lax.dot_general(
        pre_grad, up_part, (((1,), (1,)), ((), ())), preferred_element_type=jnp.float32
    )
    dx_low = dx_terms.astype(jnp.bfloat16)
    gate_low = jnp.pad(gate_terms.astype(jnp.bfloat16)[:, None], ((0, 0), (0, 127)))
    terms = jnp.concatenate([dx_low, gate_low], axis=1)
    terms = terms.reshape(chunk.shape[:-1] + (terms.shape[-1],))
    grad_down = lax.dot_general(
        hidden, scaled, (((0,), (0,)), ((), ())), preferred_element_type=jnp.float32
    )
    grad_up = lax.dot_general(
        flat_x, pre_grad, (((0,), (0,)), ((), ())), preferred_element_type=jnp.float32
    )
    return terms, grad_up, grad_down


def gelu_pair(pre_act):
    inner_arg = root_two_over_pi * (pre_act + cubic_coef * pre_act * pre_act * pre_act)
    tangent = jnp.tanh(inner_arg)
    act_value = 0.5 * pre_act * (1.0 + tangent)
    act_slope = 0.5 * (1.0 + tangent) + 0.5 * pre_act * (
        1.0 - tangent * tangent
    ) * root_two_over_pi * (1.0 + 3.0 * cubic_coef * pre_act * pre_act)
    return (act_value, act_slope)


def on_device(tokens_in, out_grad, chosen, counts, gates, w_up, w_down):
    tok_local = tokens_in.shape[0]
    width = tokens_in.shape[1]
    owners = lax.axis_size("expert")
    groups = lax.axis_size("dp")
    capacity = chosen.shape[2]
    half_cap = capacity // 2
    num_experts = chosen.shape[1]
    device = lax.axis_index("expert")
    expert = device // 2
    parity = device % 2
    my_lists = chosen[0]
    slot_ids = jnp.arange(capacity, dtype=jnp.int32)
    is_valid = slot_ids[None, :] < counts[0][:, None]
    owner_of = my_lists // tok_local
    local_of = my_lists % tok_local
    mine = jnp.logical_and(owner_of == device, is_valid)
    local_ids = jnp.arange(tok_local, dtype=jnp.int32)
    hits = jnp.logical_and(mine[:, :, None], local_of[:, :, None] == local_ids[None, None, :])
    hits_f = hits.astype(jnp.float32)
    picked = jnp.stack(
        [jnp.sum(hits_f[:, :half_cap], axis=1), jnp.sum(hits_f[:, half_cap:], axis=1)], axis=1
    )
    picked_low = picked.astype(jnp.bfloat16)
    list_row = lax.dynamic_index_in_dim(my_lists, expert, 0, keepdims=False)
    count_here = lax.dynamic_index_in_dim(counts[0], expert, 0, keepdims=False)
    valid_here = slot_ids < count_here
    gate_here = jnp.where(
        valid_here,
        lax.dynamic_index_in_dim(gates[0], expert, 0, keepdims=False),
        jnp.zeros((), jnp.bfloat16),
    )
    owner_ids = jnp.arange(owners, dtype=jnp.int32)
    slot_map = jnp.logical_and(
        (list_row // tok_local)[:, None] == owner_ids[None, :], valid_here[:, None]
    )
    slot_map = slot_map.astype(jnp.float32).reshape(2, half_cap, owners)
    map_low = slot_map.astype(jnp.bfloat16)
    gate_rows = gate_here.reshape(2, half_cap)
    both = jnp.stack([tokens_in, out_grad], axis=1)
    mine_halves = mine.reshape(num_experts, 2, half_cap)
    local_halves = local_of.reshape(num_experts, 2, half_cap)
    has_row = jnp.any(mine_halves, axis=2).reshape(owners)
    row_ids = jnp.sum(jnp.where(mine_halves, local_halves, 0), axis=2).reshape(owners)
    send_xg = jnp.take(both, row_ids, axis=0, mode="clip")
    send_xg = jnp.where(has_row[:, None, None], send_xg, jnp.zeros((), jnp.bfloat16))
    recv_xg = lax.all_to_all(send_xg, "expert", split_axis=0, concat_axis=0, tiled=True)
    map_mine = lax.dynamic_index_in_dim(map_low, parity, 0, keepdims=False)
    rows_mine = jnp.einsum(
        "ij,jsd->isd", map_mine, recv_xg, preferred_element_type=jnp.float32
    ).astype(jnp.bfloat16)
    rows_mine = rows_mine.reshape(half_cap, 2 * width)
    gate_mine = lax.dynamic_index_in_dim(gate_rows, parity, 0, keepdims=False)
    gate_col = jnp.pad(gate_mine[:, None], ((0, 0), (0, 127)))
    packed = jnp.concatenate([rows_mine, gate_col], axis=1)
    mine_rows, their_rows = dp_all_gather(packed, groups, owners)
    up_part = w_up[0]
    down_part = w_down[0]
    keep, up_mine, down_mine = expert_math(mine_rows, up_part, down_part)
    keep, their_rows = lax.optimization_barrier((keep, their_rows))
    give, up_theirs, down_theirs = expert_math(their_rows, up_part, down_part)
    got = partner(give, "dp", 0)
    got, up_mine, down_mine = lax.optimization_barrier((got, up_mine, down_mine))
    grad_up = up_mine + up_theirs
    grad_down = down_mine + down_theirs
    pieces = dp_reduce_scatter(keep, got, groups, owners)
    dx_pieces = pieces[:, :, :width].reshape(groups, half_cap, 2, width // 2)
    spread = jnp.einsum(
        "ij,kisd->jsd", map_mine, dx_pieces, preferred_element_type=jnp.float32
    ).astype(jnp.bfloat16)
    returned = lax.all_to_all(spread, "expert", split_axis=0, concat_axis=0, tiled=True)
    take_back = picked_low.reshape(owners, tok_local)
    in_grad = jnp.einsum(
        "kl,ksd->lsd", take_back, returned, preferred_element_type=jnp.float32
    )
    in_grad = in_grad.reshape(tok_local, width)
    gate_out = jnp.sum(pieces[:, :, width].astype(jnp.float32), axis=0).reshape(1, 1, half_cap)
    return (
        in_grad.astype(jnp.bfloat16),
        grad_up.astype(jnp.bfloat16)[None],
        grad_down.astype(jnp.bfloat16)[None],
        gate_out,
    )


def solution(mesh):
    placed = (
        P(("dp", "expert"), None),
        P(("dp", "expert"), None),
        P("dp", None, None),
        P("dp", None),
        P("dp", None, None),
        P("expert", None, "dp"),
        P("expert", "dp", None),
    )
    return jax.shard_map(
        on_device,
        mesh=mesh,
        in_specs=placed,
        out_specs=(
            P(("dp", "expert"), None),
            P("expert", None, "dp"),
            P("expert", "dp", None),
            P("dp", "expert", None),
        ),
        check_vma=False,
    )
```
